512 devices in a mesh: band: 32 (over x, z_lo), grid: 16 (over z_hi, y, core).
Axes of the slice: x: 4, y: 4, z: 16 (z_hi: 2, z_lo: 8; z = z_hi * 8 + z_lo), core: 2. Of those that a mesh axis runs over, the one named last changes fastest.
Arguments:
- trial_bands: float32 [64, 160, 32, 128], P('band', 'grid'), may hold values from -6 to 6
- potential: float32 [160, 32, 128], P('grid'), may hold values from -2 to 0
Outputs:
- filtered: float32 [64, 160, 32, 128], P('band', 'grid')
- projected: float32 [64, 64], P('band')
- residual_norms: float32 [64], P('band')
The draws below stay inside these ranges and needn't reach their ends.
All inputs are finite; a program needn't handle non-finite values.
Results may differ from the reference program's by a relative error of at most 0.00016.
Values sent between devices are 32-bit elements; how exact they have to be, the bound alone decides.
No kernel may reach another device: no remote copies, remote signals or barrier semaphores. Data moves between devices by JAX's collectives and lax.ppermute only.
A program may use at most 64 MiB of HBM per device.

```python
import jax
import jax.numpy as jnp
from jax import lax

NX = 32
NY = 128
BANDS = 64
NZ = 160


def level_of(stream_key, shape, pieces, smallest, largest):
    loudness, own = 1.0, jax.random.fold_in(stream_key, 6)
    for position, parts in pieces:
        steps = jnp.exp(jax.random.uniform(jax.random.fold_in(own, position), (parts,), jnp.float32, smallest / len(pieces), largest / len(pieces)))
        loudness = loudness * jnp.repeat(steps, shape[position] // parts).reshape([-1 if axis == position else 1 for axis in range(len(shape))])
    return loudness


def centred(own_key, shape, width, most, cuts=(), kind=jnp.bfloat16):
    values = width * jax.random.normal(own_key, shape, jnp.float32)
    if cuts:
        values = values * level_of(own_key, shape, cuts, -0.22, 0.18)
    return jnp.clip(values, -most, most).astype(kind)


def setup_inputs(seed: int = 0) -> dict:
    splits = jax.random.split(jax.random.key(seed), 3)
    return {
        "trial_bands": centred(splits[0], (BANDS, NZ, NX, NY), 1.0, 6.0, ((0, 32), (1, 16)), jnp.float32),
        "potential": jnp.clip(-2.0 + 2.0 * jax.random.uniform(splits[1], (NZ, NX, NY), jnp.float32) ** level_of(splits[1], (NZ, NX, NY), ((0, 16),), -0.2, 0.2), -2.0, 0.0),
    }


CENTER = 4.25
HALF_WIDTH = 3.75
LOWEST = -2.0
SIGMA_ONE = HALF_WIDTH / (LOWEST - CENTER)
FOUR_THIRDS = 4.0 / 3.0
TWELFTH = 1.0 / 12.0
filter_degree = 4

def hamiltonian(field_in, potential):
    near_sum = jnp.roll(field_in, 1, 1) + jnp.roll(field_in, -1, 1)
    near_sum = near_sum + jnp.roll(field_in, 1, 2) + jnp.roll(field_in, -1, 2)
    near_sum = near_sum + jnp.roll(field_in, 1, 3) + jnp.roll(field_in, -1, 3)
    far_sum = jnp.roll(field_in, 2, 1) + jnp.roll(field_in, -2, 1)
    far_sum = far_sum + jnp.roll(field_in, 2, 2) + jnp.roll(field_in, -2, 2)
    far_sum = far_sum + jnp.roll(field_in, 2, 3) + jnp.roll(field_in, -2, 3)
    kinetic = 0.5 * (7.5 * field_in - FOUR_THIRDS * near_sum + TWELFTH * far_sum)
    return kinetic + potential * field_in

def chebyshev(start_block, operate):
    sigma_now = SIGMA_ONE
    previous = start_block
    current = (operate(start_block) - CENTER * start_block) * (SIGMA_ONE / HALF_WIDTH)
    for repeat_index in range(filter_degree - 1):
        sigma_next = 1.0 / (2.0 / SIGMA_ONE - sigma_now)
        following = (operate(current) - CENTER * current) * (2.0 * sigma_next / HALF_WIDTH) - sigma_now * sigma_next * previous
        previous, current, sigma_now = (current, following, sigma_next)
    return current

def reference(trial_bands, potential):

    def operate(field_in):
        return hamiltonian(field_in, potential)
    filtered = chebyshev(trial_bands, operate)
    applied = operate(filtered)
    flat_bands = filtered.reshape(BANDS, -1)
    flat_image = applied.reshape(BANDS, -1)
    inverse_cells = 1.0 / (NZ * NX * NY)
    margin = jnp.dot(flat_bands.astype(jnp.float32), flat_bands.T.astype(jnp.float32), precision=lax.Precision.HIGHEST, preferred_element_type=jnp.float32) * inverse_cells
    subspace = jnp.dot(flat_image.astype(jnp.float32), flat_bands.T.astype(jnp.float32), precision=lax.Precision.HIGHEST, preferred_element_type=jnp.float32) * inverse_cells
    image_norms = jnp.sum(flat_image * flat_image, axis=1) * inverse_cells
    factor = jnp.linalg.cholesky(margin)
    coefficients = lax.linalg.triangular_solve(factor, subspace.T, left_side=True, lower=True)
    projected = lax.linalg.triangular_solve(factor, coefficients.T, left_side=True, lower=True)
    residual_norms = image_norms - jnp.sum(coefficients * coefficients, axis=0)
    return (filtered, projected, residual_norms)
```

```python
import jax
import jax.numpy as jnp
from jax import lax
from jax.sharding import PartitionSpec as P

CENTER = 4.25
HALF_WIDTH = 3.75
LOWEST = -2.0
SIGMA_ONE = HALF_WIDTH / (LOWEST - CENTER)
FOUR_THIRDS = 4.0 / 3.0
TWELFTH = 1.0 / 12.0
filter_degree = 4


def padded_2(cells, sides, width):
    for axis, dim in sides:
        count = lax.axis_size(axis)
        head = lax.slice_in_dim(cells, 0, width, axis=dim)
        tail = lax.slice_in_dim(cells, cells.shape[dim] - width, cells.shape[dim], axis=dim)
        cells = jnp.concatenate(
            [
                lax.ppermute(tail, axis, [(i, (i + 1) % count) for i in range(count)]),
                cells,
                lax.ppermute(head, axis, [((i + 1) % count, i) for i in range(count)]),
            ],
            axis=dim,
        )
    return cells


def operate(field_in, potential):
    padded = padded_2(field_in, (("grid", 1),), 2)
    plane_count = field_in.shape[1]
    near_sum = padded[:, 1 : 1 + plane_count] + padded[:, 3 : 3 + plane_count]
    near_sum = near_sum + jnp.roll(field_in, 1, 2) + jnp.roll(field_in, -1, 2)
    near_sum = near_sum + jnp.roll(field_in, 1, 3) + jnp.roll(field_in, -1, 3)
    far_sum = padded[:, 0:plane_count] + padded[:, 4 : 4 + plane_count]
    far_sum = far_sum + jnp.roll(field_in, 2, 2) + jnp.roll(field_in, -2, 2)
    far_sum = far_sum + jnp.roll(field_in, 2, 3) + jnp.roll(field_in, -2, 3)
    kinetic = 0.5 * (7.5 * field_in - FOUR_THIRDS * near_sum + TWELFTH * far_sum)
    return kinetic + potential * field_in


def on_device(trial_bands, potential):
    sigma_now = SIGMA_ONE
    previous = trial_bands
    current = (operate(trial_bands, potential) - CENTER * trial_bands) * (SIGMA_ONE / HALF_WIDTH)
    for repeat_index in range(filter_degree - 1):
        sigma_next = 1.0 / (2.0 / SIGMA_ONE - sigma_now)
        following = (operate(current, potential) - CENTER * current) * (
            2.0 * sigma_next / HALF_WIDTH
        ) - sigma_now * sigma_next * previous
        previous, current, sigma_now = (current, following, sigma_next)
    applied = operate(current, potential)
    band_count = current.shape[0]
    band_devices = lax.axis_size("band")
    total_bands = band_count * band_devices
    cell_count = current.shape[1] * current.shape[2] * current.shape[3]
    cell_total = cell_count * lax.axis_size("grid")
    inverse_cells = 1.0 / cell_total
    first_band = lax.axis_index("band") * band_count
    both = jnp.stack(
        [current.reshape(band_count, cell_count), applied.reshape(band_count, cell_count)]
    ).reshape(2, band_count, band_devices, cell_count // band_devices)
    moved = lax.all_to_all(both, "band", 2, 1, tiled=True)
    bands_here = moved[0].reshape(total_bands, -1)
    image_here = moved[1].reshape(total_bands, -1)
    margin_part = jnp.dot(
        bands_here, bands_here.T, precision=lax.Precision.HIGHEST, preferred_element_type=jnp.float32
    )
    image_part = jnp.dot(
        image_here, bands_here.T, precision=lax.Precision.HIGHEST, preferred_element_type=jnp.float32
    )
    norm_part = jnp.sum(image_here * image_here, axis=1)
    packed = jnp.concatenate([margin_part.reshape(-1), image_part.reshape(-1), norm_part])
    packed = lax.psum(packed, ("band", "grid")) * inverse_cells
    square = total_bands * total_bands
    margin = packed[:square].reshape(total_bands, total_bands)
    subspace = packed[square : 2 * square].reshape(total_bands, total_bands)
    image_norms = packed[2 * square :]
    factor = jnp.linalg.cholesky(margin)
    coefficients = lax.linalg.triangular_solve(factor, subspace.T, left_side=True, lower=True)
    projected = lax.linalg.triangular_solve(factor, coefficients.T, left_side=True, lower=True)
    residual_norms = image_norms - jnp.sum(coefficients * coefficients, axis=0)
    projected_rows = lax.dynamic_slice_in_dim(projected, first_band, band_count, 0)
    residual_rows = lax.dynamic_slice_in_dim(residual_norms, first_band, band_count, 0)
    return (current, projected_rows, residual_rows)


def solution(mesh):
    in_specs = (P("band", "grid", None, None), P("grid", None, None))
    out_specs = (P("band", "grid", None, None), P("band", None), P("band"))
    return jax.shard_map(
        on_device, mesh=mesh, in_specs=in_specs, out_specs=out_specs, check_vma=False
    )
```

```python
import jax
import jax.numpy as jnp
from jax import lax
from jax.sharding import PartitionSpec as P

CENTER = 4.25
HALF_WIDTH = 3.75
LOWEST = -2.0
SIGMA_ONE = HALF_WIDTH / (LOWEST - CENTER)
FOUR_THIRDS = 4.0 / 3.0
TWELFTH = 1.0 / 12.0
filter_degree = 4


def padded_2(cells, sides, width):
    for axis, dim in sides:
        count = lax.axis_size(axis)
        head = lax.slice_in_dim(cells, 0, width, axis=dim)
        tail = lax.slice_in_dim(cells, cells.shape[dim] - width, cells.shape[dim], axis=dim)
        cells = jnp.concatenate(
            [
                lax.ppermute(tail, axis, [(i, (i + 1) % count) for i in range(count)]),
                cells,
                lax.ppermute(head, axis, [((i + 1) % count, i) for i in range(count)]),
            ],
            axis=dim,
        )
    return cells


def butterfly_sum(values, axis):
    count = lax.axis_size(axis)
    step = 1
    while step < count:
        values = values + lax.ppermute(values, axis, [(i, i ^ step) for i in range(count)])
        step *= 2
    return values


def operate(field_in, potential):
    padded = padded_2(field_in, (("grid", 1),), 2)
    plane_count = field_in.shape[1]
    near_sum = padded[:, 1 : 1 + plane_count] + padded[:, 3 : 3 + plane_count]
    near_sum = near_sum + jnp.roll(field_in, 1, 2) + jnp.roll(field_in, -1, 2)
    near_sum = near_sum + jnp.roll(field_in, 1, 3) + jnp.roll(field_in, -1, 3)
    far_sum = padded[:, 0:plane_count] + padded[:, 4 : 4 + plane_count]
    far_sum = far_sum + jnp.roll(field_in, 2, 2) + jnp.roll(field_in, -2, 2)
    far_sum = far_sum + jnp.roll(field_in, 2, 3) + jnp.roll(field_in, -2, 3)
    kinetic = 0.5 * (7.5 * field_in - FOUR_THIRDS * near_sum + TWELFTH * far_sum)
    return kinetic + potential * field_in


def on_device(trial_bands, potential):
    sigma_now = SIGMA_ONE
    previous = trial_bands
    current = (operate(trial_bands, potential) - CENTER * trial_bands) * (SIGMA_ONE / HALF_WIDTH)
    for repeat_index in range(filter_degree - 1):
        sigma_next = 1.0 / (2.0 / SIGMA_ONE - sigma_now)
        following = (operate(current, potential) - CENTER * current) * (
            2.0 * sigma_next / HALF_WIDTH
        ) - sigma_now * sigma_next * previous
        previous, current, sigma_now = (current, following, sigma_next)
    applied = operate(current, potential)
    band_count = current.shape[0]
    band_devices = lax.axis_size("band")
    total_bands = band_count * band_devices
    cell_count = current.shape[1] * current.shape[2] * current.shape[3]
    cell_total = cell_count * lax.axis_size("grid")
    inverse_cells = 1.0 / cell_total
    first_band = lax.axis_index("band") * band_count
    both = jnp.stack(
        [current.reshape(band_count, cell_count), applied.reshape(band_count, cell_count)]
    ).reshape(2, band_count, band_devices, cell_count // band_devices)
    moved = lax.all_to_all(both, "band", 2, 1, tiled=True)
    bands_here = moved[0].reshape(total_bands, -1)
    image_here = moved[1].reshape(total_bands, -1)
    margin_part = jnp.dot(
        bands_here, bands_here.T, precision=lax.Precision.HIGHEST, preferred_element_type=jnp.float32
    )
    image_part = jnp.dot(
        image_here, bands_here.T, precision=lax.Precision.HIGHEST, preferred_element_type=jnp.float32
    )
    norm_part = jnp.sum(image_here * image_here, axis=1)
    packed = jnp.concatenate([margin_part.reshape(-1), image_part.reshape(-1), norm_part])
    packed = butterfly_sum(butterfly_sum(packed, "grid"), "band") * inverse_cells
    square = total_bands * total_bands
    margin = packed[:square].reshape(total_bands, total_bands)
    subspace = packed[square : 2 * square].reshape(total_bands, total_bands)
    image_norms = packed[2 * square :]
    factor = jnp.linalg.cholesky(margin)
    coefficients = lax.linalg.triangular_solve(factor, subspace.T, left_side=True, lower=True)
    projected = lax.linalg.triangular_solve(factor, coefficients.T, left_side=True, lower=True)
    residual_norms = image_norms - jnp.sum(coefficients * coefficients, axis=0)
    projected_rows = lax.dynamic_slice_in_dim(projected, first_band, band_count, 0)
    residual_rows = lax.dynamic_slice_in_dim(residual_norms, first_band, band_count, 0)
    return (current, projected_rows, residual_rows)


def solution(mesh):
    in_specs = (P("band", "grid", None, None), P("grid", None, None))
    out_specs = (P("band", "grid", None, None), P("band", None), P("band"))
    return jax.shard_map(
        on_device, mesh=mesh, in_specs=in_specs, out_specs=out_specs, check_vma=False
    )
```

```python
import jax
import jax.numpy as jnp
from jax import lax
from jax.sharding import PartitionSpec as P

CENTER = 4.25
HALF_WIDTH = 3.75
LOWEST = -2.0
SIGMA_ONE = HALF_WIDTH / (LOWEST - CENTER)
FOUR_THIRDS = 4.0 / 3.0
TWELFTH = 1.0 / 12.0
filter_degree = 4


def butterfly_sum(values, axis):
    count = lax.axis_size(axis)
    step = 1
    while step < count:
        values = values + lax.ppermute(values, axis, [(i, i ^ step) for i in range(count)])
        step *= 2
    return values


def widened(cells, width):
    count = lax.axis_size("grid")
    head = cells[:, :width]
    tail = cells[:, cells.shape[1] - width :]
    return jnp.concatenate(
        [
            lax.ppermute(tail, "grid", [(i, (i + 1) % count) for i in range(count)]),
            cells,
            lax.ppermute(head, "grid", [((i + 1) % count, i) for i in range(count)]),
        ],
        axis=1,
    )


def operate(field_in, potential):
    plane_count = field_in.shape[1] - 4
    centre = field_in[:, 2 : 2 + plane_count]
    near_sum = field_in[:, 1 : 1 + plane_count] + field_in[:, 3 : 3 + plane_count]
    near_sum = near_sum + jnp.roll(centre, 1, 2) + jnp.roll(centre, -1, 2)
    near_sum = near_sum + jnp.roll(centre, 1, 3) + jnp.roll(centre, -1, 3)
    far_sum = field_in[:, 0:plane_count] + field_in[:, 4 : 4 + plane_count]
    far_sum = far_sum + jnp.roll(centre, 2, 2) + jnp.roll(centre, -2, 2)
    far_sum = far_sum + jnp.roll(centre, 2, 3) + jnp.roll(centre, -2, 3)
    kinetic = 0.5 * (7.5 * centre - FOUR_THIRDS * near_sum + TWELFTH * far_sum)
    return kinetic + potential * centre


def on_device(trial_bands, potential):
    band_count, own_planes = trial_bands.shape[0], trial_bands.shape[1]
    width = 2 * (filter_degree + 1)
    payload = jnp.concatenate([trial_bands, potential[None]], axis=0)
    wide = widened(payload, width)
    wide_bands, wide_potential = wide[:band_count], wide[band_count]
    offset = [0]

    def step(field_in):
        first = offset[0] + 2
        result = operate(field_in, wide_potential[first : first + field_in.shape[1] - 4])
        return result, first

    def trim(values, at, first, count):
        return values[:, first - at : first - at + count]

    sigma_now = SIGMA_ONE
    previous, previous_at = wide_bands, 0
    image_in, first = step(wide_bands)
    current = (image_in - CENTER * trim(wide_bands, 0, first, image_in.shape[1])) * (SIGMA_ONE / HALF_WIDTH)
    current_at = first
    for repeat_index in range(filter_degree - 1):
        sigma_next = 1.0 / (2.0 / SIGMA_ONE - sigma_now)
        offset[0] = current_at
        image_in, first = step(current)
        count = image_in.shape[1]
        following = (image_in - CENTER * trim(current, current_at, first, count)) * (
            2.0 * sigma_next / HALF_WIDTH
        ) - sigma_now * sigma_next * trim(previous, previous_at, first, count)
        previous, previous_at = current, current_at
        current, current_at, sigma_now = following, first, sigma_next
    offset[0] = current_at
    applied, first = step(current)
    current = trim(current, current_at, first, own_planes)
    band_devices = lax.axis_size("band")
    total_bands = band_count * band_devices
    cell_count = current.shape[1] * current.shape[2] * current.shape[3]
    cell_total = cell_count * lax.axis_size("grid")
    inverse_cells = 1.0 / cell_total
    first_band = lax.axis_index("band") * band_count
    both = jnp.stack(
        [current.reshape(band_count, cell_count), applied.reshape(band_count, cell_count)]
    ).reshape(2, band_count, band_devices, cell_count // band_devices)
    moved = lax.all_to_all(both, "band", 2, 1, tiled=True)
    bands_here = moved[0].reshape(total_bands, -1)
    image_here = moved[1].reshape(total_bands, -1)
    margin_part = jnp.dot(
        bands_here, bands_here.T, precision=lax.Precision.HIGHEST, preferred_element_type=jnp.float32
    )
    image_part = jnp.dot(
        image_here, bands_here.T, precision=lax.Precision.HIGHEST, preferred_element_type=jnp.float32
    )
    norm_part = jnp.sum(image_here * image_here, axis=1)
    packed = jnp.concatenate([margin_part.reshape(-1), image_part.reshape(-1), norm_part])
    packed = butterfly_sum(butterfly_sum(packed, "grid"), "band") * inverse_cells
    square = total_bands * total_bands
    margin = packed[:square].reshape(total_bands, total_bands)
    subspace = packed[square : 2 * square].reshape(total_bands, total_bands)
    image_norms = packed[2 * square :]
    factor = jnp.linalg.cholesky(margin)
    coefficients = lax.linalg.triangular_solve(factor, subspace.T, left_side=True, lower=True)
    projected = lax.linalg.triangular_solve(factor, coefficients.T, left_side=True, lower=True)
    residual_norms = image_norms - jnp.sum(coefficients * coefficients, axis=0)
    projected_rows = lax.dynamic_slice_in_dim(projected, first_band, band_count, 0)
    residual_rows = lax.dynamic_slice_in_dim(residual_norms, first_band, band_count, 0)
    return (current, projected_rows, residual_rows)


def solution(mesh):
    in_specs = (P("band", "grid", None, None), P("grid", None, None))
    out_specs = (P("band", "grid", None, None), P("band", None), P("band"))
    return jax.shard_map(
        on_device, mesh=mesh, in_specs=in_specs, out_specs=out_specs, check_vma=False
    )
```

```python
import jax
import jax.numpy as jnp
from jax import lax
from jax.sharding import PartitionSpec as P

CENTER = 4.25
HALF_WIDTH = 3.75
LOWEST = -2.0
SIGMA_ONE = HALF_WIDTH / (LOWEST - CENTER)
FOUR_THIRDS = 4.0 / 3.0
TWELFTH = 1.0 / 12.0
filter_degree = 4


def butterfly_sum(values, axis, partner_rounds):
    count = lax.axis_size(axis)
    for partner in partner_rounds:
        pairs = [(i, partner(i)) for i in range(count)]
        values = values + lax.ppermute(values, axis, pairs)
    return values


def flip(bit):
    return lambda i: i ^ bit


def ring_of_four(low, stride):
    def partner(i):
        place = (i // stride) % 4
        return i + (3 - 2 * place) * stride

    return partner


def widened(cells, width):
    count = lax.axis_size("grid")
    head = cells[:, :width]
    tail = cells[:, cells.shape[1] - width :]
    return jnp.concatenate(
        [
            lax.ppermute(tail, "grid", [(i, (i + 1) % count) for i in range(count)]),
            cells,
            lax.ppermute(head, "grid", [((i + 1) % count, i) for i in range(count)]),
        ],
        axis=1,
    )


def operate(field_in, potential):
    plane_count = field_in.shape[1] - 4
    centre = field_in[:, 2 : 2 + plane_count]
    near_sum = field_in[:, 1 : 1 + plane_count] + field_in[:, 3 : 3 + plane_count]
    near_sum = near_sum + jnp.roll(centre, 1, 2) + jnp.roll(centre, -1, 2)
    near_sum = near_sum + jnp.roll(centre, 1, 3) + jnp.roll(centre, -1, 3)
    far_sum = field_in[:, 0:plane_count] + field_in[:, 4 : 4 + plane_count]
    far_sum = far_sum + jnp.roll(centre, 2, 2) + jnp.roll(centre, -2, 2)
    far_sum = far_sum + jnp.roll(centre, 2, 3) + jnp.roll(centre, -2, 3)
    kinetic = 0.5 * (7.5 * centre - FOUR_THIRDS * near_sum + TWELFTH * far_sum)
    return kinetic + potential * centre


def on_device(trial_bands, potential):
    band_count, own_planes = trial_bands.shape[0], trial_bands.shape[1]
    width = 2 * (filter_degree + 1)
    payload = jnp.concatenate([trial_bands, potential[None]], axis=0)
    wide = widened(payload, width)
    wide_bands, wide_potential = wide[:band_count], wide[band_count]
    offset = [0]

    def step(field_in):
        first = offset[0] + 2
        result = operate(field_in, wide_potential[first : first + field_in.shape[1] - 4])
        return result, first

    def trim(values, at, first, count):
        return values[:, first - at : first - at + count]

    sigma_now = SIGMA_ONE
    previous, previous_at = wide_bands, 0
    image_in, first = step(wide_bands)
    current = (image_in - CENTER * trim(wide_bands, 0, first, image_in.shape[1])) * (SIGMA_ONE / HALF_WIDTH)
    current_at = first
    for repeat_index in range(filter_degree - 1):
        sigma_next = 1.0 / (2.0 / SIGMA_ONE - sigma_now)
        offset[0] = current_at
        image_in, first = step(current)
        count = image_in.shape[1]
        following = (image_in - CENTER * trim(current, current_at, first, count)) * (
            2.0 * sigma_next / HALF_WIDTH
        ) - sigma_now * sigma_next * trim(previous, previous_at, first, count)
        previous, previous_at = current, current_at
        current, current_at, sigma_now = following, first, sigma_next
    offset[0] = current_at
    applied, first = step(current)
    current = trim(current, current_at, first, own_planes)
    band_devices = lax.axis_size("band")
    total_bands = band_count * band_devices
    cell_count = current.shape[1] * current.shape[2] * current.shape[3]
    cell_total = cell_count * lax.axis_size("grid")
    inverse_cells = 1.0 / cell_total
    first_band = lax.axis_index("band") * band_count
    both = jnp.stack(
        [current.reshape(band_count, cell_count), applied.reshape(band_count, cell_count)]
    ).reshape(2, band_count, band_devices, cell_count // band_devices)
    moved = lax.all_to_all(both, "band", 2, 1, tiled=True)
    bands_here = moved[0].reshape(total_bands, -1)
    image_here = moved[1].reshape(total_bands, -1)
    margin_part = jnp.dot(
        bands_here, bands_here.T, precision=lax.Precision.HIGHEST, preferred_element_type=jnp.float32
    )
    image_part = jnp.dot(
        image_here, bands_here.T, precision=lax.Precision.HIGHEST, preferred_element_type=jnp.float32
    )
    norm_part = jnp.sum(image_here * image_here, axis=1)
    packed = jnp.concatenate([margin_part.reshape(-1), image_part.reshape(-1), norm_part])
    packed = butterfly_sum(packed, "grid", [flip(1), flip(2), ring_of_four(0, 2), flip(8)])
    packed = butterfly_sum(packed, "band", [flip(1), flip(2), flip(4), flip(8), ring_of_four(0, 8)])
    packed = packed * inverse_cells
    square = total_bands * total_bands
    margin = packed[:square].reshape(total_bands, total_bands)
    subspace = packed[square : 2 * square].reshape(total_bands, total_bands)
    image_norms = packed[2 * square :]
    factor = jnp.linalg.cholesky(margin)
    coefficients = lax.linalg.triangular_solve(factor, subspace.T, left_side=True, lower=True)
    projected = lax.linalg.triangular_solve(factor, coefficients.T, left_side=True, lower=True)
    residual_norms = image_norms - jnp.sum(coefficients * coefficients, axis=0)
    projected_rows = lax.dynamic_slice_in_dim(projected, first_band, band_count, 0)
    residual_rows = lax.dynamic_slice_in_dim(residual_norms, first_band, band_count, 0)
    return (current, projected_rows, residual_rows)


def solution(mesh):
    in_specs = (P("band", "grid", None, None), P("grid", None, None))
    out_specs = (P("band", "grid", None, None), P("band", None), P("band"))
    return jax.shard_map(
        on_device, mesh=mesh, in_specs=in_specs, out_specs=out_specs, check_vma=False
    )
```

```python
import jax
import jax.numpy as jnp
from jax import lax
from jax.experimental import pallas as pl
from jax.experimental.pallas import tpu as pltpu
from jax.sharding import PartitionSpec as P

CENTER = 4.25
HALF_WIDTH = 3.75
LOWEST = -2.0
SIGMA_ONE = HALF_WIDTH / (LOWEST - CENTER)
FOUR_THIRDS = 4.0 / 3.0
TWELFTH = 1.0 / 12.0
filter_degree = 4


def butterfly_sum(values, axis, partner_rounds):
    count = lax.axis_size(axis)
    for partner in partner_rounds:
        pairs = [(i, partner(i)) for i in range(count)]
        values = values + lax.ppermute(values, axis, pairs)
    return values


def flip(bit):
    return lambda i: i ^ bit


def ring_of_four(low, stride):
    def partner(i):
        place = (i // stride) % 4
        return i + (3 - 2 * place) * stride

    return partner


def filter_kernel(below_ref, own_ref, above_ref, filtered_ref, image_ref, first_buf, second_buf, third_buf, wide_pot):
    band_count, own_planes = filtered_ref.shape[0], filtered_ref.shape[1]
    width = below_ref.shape[1]
    for at, source in ((0, below_ref), (width, own_ref), (width + own_planes, above_ref)):
        first_buf[:, at : at + source.shape[1]] = source[:band_count]
        wide_pot[at : at + source.shape[1]] = source[band_count]
    rows, lanes = first_buf.shape[2], first_buf.shape[3]

    def apply(field, band, plane):
        centre = field[band, plane]
        near_sum = field[band, plane - 1] + field[band, plane + 1]
        near_sum = near_sum + pltpu.roll(centre, 1, 0) + pltpu.roll(centre, rows - 1, 0)
        near_sum = near_sum + pltpu.roll(centre, 1, 1) + pltpu.roll(centre, lanes - 1, 1)
        far_sum = field[band, plane - 2] + field[band, plane + 2]
        far_sum = far_sum + pltpu.roll(centre, 2, 0) + pltpu.roll(centre, rows - 2, 0)
        far_sum = far_sum + pltpu.roll(centre, 2, 1) + pltpu.roll(centre, lanes - 2, 1)
        kinetic = 0.5 * (7.5 * centre - FOUR_THIRDS * near_sum + TWELFTH * far_sum)
        return kinetic + wide_pot[plane] * centre, centre

    def sweep(field, older, out, lo, hi, scale, carry_scale):
        @pl.loop(lo, hi)
        def _(plane):
            for band in range(band_count):
                applied, centre = apply(field, band, plane)
                value = (applied - CENTER * centre) * scale
                if older is not None:
                    value = value - carry_scale * older[band, plane]
                out[band, plane] = value

    total = first_buf.shape[1]
    sweep(first_buf, None, second_buf, 2, total - 2, SIGMA_ONE / HALF_WIDTH, 0.0)
    bufs = [first_buf, second_buf, third_buf]
    older, field, spare = 0, 1, 2
    sigma_now = SIGMA_ONE
    for repeat_index in range(filter_degree - 1):
        sigma_next = 1.0 / (2.0 / SIGMA_ONE - sigma_now)
        margin = 2 * (repeat_index + 2)
        sweep(bufs[field], bufs[older], bufs[spare], margin, total - margin,
              2.0 * sigma_next / HALF_WIDTH, sigma_now * sigma_next)
        older, field, spare = field, spare, older
        sigma_now = sigma_next
    final = bufs[field]
    filtered_ref[...] = final[:, width : width + own_planes]

    @pl.loop(width, width + own_planes)
    def _(plane):
        for band in range(band_count):
            image_ref[band, plane - width], _ = apply(final, band, plane)


def filter_and_image(below, own, above):
    band_count = own.shape[0] - 1
    own_planes, rows, lanes = own.shape[1], own.shape[2], own.shape[3]
    total = below.shape[1] + own_planes + above.shape[1]
    shape = (band_count, own_planes, rows, lanes)
    cells = band_count * total * rows * lanes
    return pl.pallas_call(
        filter_kernel,
        out_shape=(jax.ShapeDtypeStruct(shape, jnp.float32), jax.ShapeDtypeStruct(shape, jnp.float32)),
        in_specs=[pl.BlockSpec(memory_space=pltpu.VMEM)] * 3,
        out_specs=(pl.BlockSpec(memory_space=pltpu.VMEM), pl.BlockSpec(memory_space=pltpu.VMEM)),
        scratch_shapes=[pltpu.VMEM((band_count, total, rows, lanes), jnp.float32)] * 3
        + [pltpu.VMEM((total, rows, lanes), jnp.float32)],
        cost_estimate=pl.CostEstimate(flops=30 * cells * 4, transcendentals=0, bytes_accessed=4 * cells * 3),
    )(below, own, above)


def on_device(trial_bands, potential):
    band_count = trial_bands.shape[0]
    width = 2 * (filter_degree + 1)
    count = lax.axis_size("grid")
    payload = jnp.concatenate([trial_bands, potential[None]], axis=0)
    below = lax.ppermute(payload[:, payload.shape[1] - width :], "grid", [(i, (i + 1) % count) for i in range(count)])
    above = lax.ppermute(payload[:, :width], "grid", [((i + 1) % count, i) for i in range(count)])
    current, applied = filter_and_image(below, payload, above)
    band_devices = lax.axis_size("band")
    total_bands = band_count * band_devices
    cell_count = current.shape[1] * current.shape[2] * current.shape[3]
    cell_total = cell_count * lax.axis_size("grid")
    inverse_cells = 1.0 / cell_total
    first_band = lax.axis_index("band") * band_count
    both = jnp.stack(
        [current.reshape(band_count, cell_count), applied.reshape(band_count, cell_count)]
    ).reshape(2, band_count, band_devices, cell_count // band_devices)
    moved = lax.all_to_all(both, "band", 2, 1, tiled=True)
    bands_here = moved[0].reshape(total_bands, -1)
    image_here = moved[1].reshape(total_bands, -1)
    margin_part = jnp.dot(
        bands_here, bands_here.T, precision=lax.Precision.HIGHEST, preferred_element_type=jnp.float32
    )
    image_part = jnp.dot(
        image_here, bands_here.T, precision=lax.Precision.HIGHEST, preferred_element_type=jnp.float32
    )
    norm_part = jnp.sum(image_here * image_here, axis=1)
    packed = jnp.concatenate([margin_part.reshape(-1), image_part.reshape(-1), norm_part])
    packed = butterfly_sum(packed, "grid", [flip(1), flip(2), ring_of_four(0, 2), flip(8)])
    packed = butterfly_sum(packed, "band", [flip(1), flip(2), flip(4), flip(8), ring_of_four(0, 8)])
    packed = packed * inverse_cells
    square = total_bands * total_bands
    margin = packed[:square].reshape(total_bands, total_bands)
    subspace = packed[square : 2 * square].reshape(total_bands, total_bands)
    image_norms = packed[2 * square :]
    factor = jnp.linalg.cholesky(margin)
    coefficients = lax.linalg.triangular_solve(factor, subspace.T, left_side=True, lower=True)
    projected = lax.linalg.triangular_solve(factor, coefficients.T, left_side=True, lower=True)
    residual_norms = image_norms - jnp.sum(coefficients * coefficients, axis=0)
    projected_rows = lax.dynamic_slice_in_dim(projected, first_band, band_count, 0)
    residual_rows = lax.dynamic_slice_in_dim(residual_norms, first_band, band_count, 0)
    return (current, projected_rows, residual_rows)


def solution(mesh):
    in_specs = (P("band", "grid", None, None), P("grid", None, None))
    out_specs = (P("band", "grid", None, None), P("band", None), P("band"))
    return jax.shard_map(
        on_device, mesh=mesh, in_specs=in_specs, out_specs=out_specs, check_vma=False
    )
```

```python
import jax
import jax.numpy as jnp
from jax import lax
from jax.experimental import pallas as pl
from jax.experimental.pallas import tpu as pltpu
from jax.sharding import PartitionSpec as P

CENTER = 4.25
HALF_WIDTH = 3.75
LOWEST = -2.0
SIGMA_ONE = HALF_WIDTH / (LOWEST - CENTER)
FOUR_THIRDS = 4.0 / 3.0
TWELFTH = 1.0 / 12.0
filter_degree = 4


def butterfly_sum(values, axis, partner_rounds):
    count = lax.axis_size(axis)
    for partner in partner_rounds:
        pairs = [(i, partner(i)) for i in range(count)]
        values = values + lax.ppermute(values, axis, pairs)
    return values


def flip(bit):
    return lambda i: i ^ bit


def ring_of_four(low, stride):
    def partner(i):
        place = (i // stride) % 4
        return i + (3 - 2 * place) * stride

    return partner


def filter_kernel(below_ref, own_ref, above_ref, below_pot, own_pot, above_pot, filtered_ref, image_ref,
                  first_buf, second_buf, third_buf, wide_pot):
    band_count, own_planes = filtered_ref.shape[0], filtered_ref.shape[1]
    width = below_ref.shape[1]
    for at, source, pot in ((0, below_ref, below_pot), (width, own_ref, own_pot),
                            (width + own_planes, above_ref, above_pot)):
        first_buf[:, at : at + source.shape[1]] = source[...]
        wide_pot[at : at + source.shape[1]] = pot[...]
    rows, lanes = first_buf.shape[2], first_buf.shape[3]

    def apply(field, band, plane):
        centre = field[band, plane]
        near_sum = field[band, plane - 1] + field[band, plane + 1]
        near_sum = near_sum + pltpu.roll(centre, 1, 0) + pltpu.roll(centre, rows - 1, 0)
        near_sum = near_sum + pltpu.roll(centre, 1, 1) + pltpu.roll(centre, lanes - 1, 1)
        far_sum = field[band, plane - 2] + field[band, plane + 2]
        far_sum = far_sum + pltpu.roll(centre, 2, 0) + pltpu.roll(centre, rows - 2, 0)
        far_sum = far_sum + pltpu.roll(centre, 2, 1) + pltpu.roll(centre, lanes - 2, 1)
        kinetic = 0.5 * (7.5 * centre - FOUR_THIRDS * near_sum + TWELFTH * far_sum)
        return kinetic + wide_pot[plane] * centre, centre

    def sweep(field, older, out, lo, hi, scale, carry_scale):
        @pl.loop(lo, hi)
        def _(plane):
            for band in range(band_count):
                applied, centre = apply(field, band, plane)
                value = (applied - CENTER * centre) * scale
                if older is not None:
                    value = value - carry_scale * older[band, plane]
                out[band, plane] = value

    total = first_buf.shape[1]
    sweep(first_buf, None, second_buf, 2, total - 2, SIGMA_ONE / HALF_WIDTH, 0.0)
    bufs = [first_buf, second_buf, third_buf]
    older, field, spare = 0, 1, 2
    sigma_now = SIGMA_ONE
    for repeat_index in range(filter_degree - 1):
        sigma_next = 1.0 / (2.0 / SIGMA_ONE - sigma_now)
        margin = 2 * (repeat_index + 2)
        sweep(bufs[field], bufs[older], bufs[spare], margin, total - margin,
              2.0 * sigma_next / HALF_WIDTH, sigma_now * sigma_next)
        older, field, spare = field, spare, older
        sigma_now = sigma_next
    final = bufs[field]
    filtered_ref[...] = final[:, width : width + own_planes]

    @pl.loop(width, width + own_planes)
    def _(plane):
        for band in range(band_count):
            image_ref[band, plane - width], _ = apply(final, band, plane)


def filter_and_image(below, own, above, below_pot, own_pot, above_pot):
    band_count = own.shape[0]
    own_planes, rows, lanes = own.shape[1], own.shape[2], own.shape[3]
    total = below.shape[1] + own_planes + above.shape[1]
    shape = (band_count, own_planes, rows, lanes)
    cells = band_count * total * rows * lanes
    return pl.pallas_call(
        filter_kernel,
        out_shape=(jax.ShapeDtypeStruct(shape, jnp.float32), jax.ShapeDtypeStruct(shape, jnp.float32)),
        in_specs=[pl.BlockSpec(memory_space=pltpu.VMEM)] * 6,
        out_specs=(pl.BlockSpec(memory_space=pltpu.VMEM), pl.BlockSpec(memory_space=pltpu.VMEM)),
        scratch_shapes=[pltpu.VMEM((band_count, total, rows, lanes), jnp.float32)] * 3
        + [pltpu.VMEM((total, rows, lanes), jnp.float32)],
        cost_estimate=pl.CostEstimate(flops=30 * cells * 4, transcendentals=0, bytes_accessed=4 * cells * 3),
    )(below, own, above, below_pot, own_pot, above_pot)


def replica_pairs(direction):
    grid_count, band_count = lax.axis_size("grid"), lax.axis_size("band")
    pairs = []
    for target_grid in range(grid_count):
        source_grid = (target_grid - direction) % grid_count
        far = source_grid // 8 != target_grid // 8
        for target_band in range(band_count):
            source_band = target_band ^ 4 if far else target_band
            pairs.append((source_band * grid_count + source_grid, target_band * grid_count + target_grid))
    return pairs


def on_device(trial_bands, potential):
    band_count = trial_bands.shape[0]
    width = 2 * (filter_degree + 1)
    count = lax.axis_size("grid")
    below = lax.ppermute(trial_bands[:, trial_bands.shape[1] - width :], "grid", [(i, (i + 1) % count) for i in range(count)])
    above = lax.ppermute(trial_bands[:, :width], "grid", [((i + 1) % count, i) for i in range(count)])
    below_pot = lax.ppermute(potential[potential.shape[0] - width :], ("band", "grid"), replica_pairs(1))
    above_pot = lax.ppermute(potential[:width], ("band", "grid"), replica_pairs(-1))
    current, applied = filter_and_image(below, trial_bands, above, below_pot, potential, above_pot)
    band_devices = lax.axis_size("band")
    total_bands = band_count * band_devices
    cell_count = current.shape[1] * current.shape[2] * current.shape[3]
    cell_total = cell_count * lax.axis_size("grid")
    inverse_cells = 1.0 / cell_total
    first_band = lax.axis_index("band") * band_count
    both = jnp.stack(
        [current.reshape(band_count, cell_count), applied.reshape(band_count, cell_count)]
    ).reshape(2, band_count, band_devices, cell_count // band_devices)
    moved = lax.all_to_all(both, "band", 2, 1, tiled=True)
    bands_here = moved[0].reshape(total_bands, -1)
    image_here = moved[1].reshape(total_bands, -1)
    margin_part = jnp.dot(
        bands_here, bands_here.T, precision=lax.Precision.HIGHEST, preferred_element_type=jnp.float32
    )
    image_part = jnp.dot(
        image_here, bands_here.T, precision=lax.Precision.HIGHEST, preferred_element_type=jnp.float32
    )
    norm_part = jnp.sum(image_here * image_here, axis=1)
    packed = jnp.concatenate([margin_part.reshape(-1), image_part.reshape(-1), norm_part])
    packed = butterfly_sum(packed, "grid", [flip(1), flip(2), ring_of_four(0, 2), flip(8)])
    packed = butterfly_sum(packed, "band", [flip(1), flip(2), flip(4), flip(8), ring_of_four(0, 8)])
    packed = packed * inverse_cells
    square = total_bands * total_bands
    margin = packed[:square].reshape(total_bands, total_bands)
    subspace = packed[square : 2 * square].reshape(total_bands, total_bands)
    image_norms = packed[2 * square :]
    factor = jnp.linalg.cholesky(margin)
    coefficients = lax.linalg.triangular_solve(factor, subspace.T, left_side=True, lower=True)
    projected = lax.linalg.triangular_solve(factor, coefficients.T, left_side=True, lower=True)
    residual_norms = image_norms - jnp.sum(coefficients * coefficients, axis=0)
    projected_rows = lax.dynamic_slice_in_dim(projected, first_band, band_count, 0)
    residual_rows = lax.dynamic_slice_in_dim(residual_norms, first_band, band_count, 0)
    return (current, projected_rows, residual_rows)


def solution(mesh):
    in_specs = (P("band", "grid", None, None), P("grid", None, None))
    out_specs = (P("band", "grid", None, None), P("band", None), P("band"))
    return jax.shard_map(
        on_device, mesh=mesh, in_specs=in_specs, out_specs=out_specs, check_vma=False
    )
```

```python
import jax
import jax.numpy as jnp
from jax import lax
from jax.experimental import pallas as pl
from jax.experimental.pallas import tpu as pltpu
from jax.sharding import PartitionSpec as P

CENTER = 4.25
HALF_WIDTH = 3.75
LOWEST = -2.0
SIGMA_ONE = HALF_WIDTH / (LOWEST - CENTER)
FOUR_THIRDS = 4.0 / 3.0
TWELFTH = 1.0 / 12.0
filter_degree = 4


def butterfly_sum(values, axis, partner_rounds):
    count = lax.axis_size(axis)
    for partner in partner_rounds:
        pairs = [(i, partner(i)) for i in range(count)]
        values = values + lax.ppermute(values, axis, pairs)
    return values


def flip(bit):
    return lambda i: i ^ bit


def ring_of_four(low, stride):
    def partner(i):
        place = (i // stride) % 4
        return i + (3 - 2 * place) * stride

    return partner


def filter_kernel(below_ref, own_ref, above_ref, below_pot, own_pot, above_pot, filtered_ref, image_ref,
                  first_buf, second_buf, third_buf, wide_pot):
    band_count, own_planes = filtered_ref.shape[0], filtered_ref.shape[1]
    width = below_ref.shape[1]
    for at, source, pot in ((0, below_ref, below_pot), (width, own_ref, own_pot),
                            (width + own_planes, above_ref, above_pot)):
        first_buf[:, at : at + source.shape[1]] = source[...]
        wide_pot[at : at + source.shape[1]] = pot[...]
    rows, lanes = first_buf.shape[2], first_buf.shape[3]

    def apply(field, band, plane):
        centre = field[band, plane]
        near_sum = field[band, plane - 1] + field[band, plane + 1]
        near_sum = near_sum + pltpu.roll(centre, 1, 0) + pltpu.roll(centre, rows - 1, 0)
        near_sum = near_sum + pltpu.roll(centre, 1, 1) + pltpu.roll(centre, lanes - 1, 1)
        far_sum = field[band, plane - 2] + field[band, plane + 2]
        far_sum = far_sum + pltpu.roll(centre, 2, 0) + pltpu.roll(centre, rows - 2, 0)
        far_sum = far_sum + pltpu.roll(centre, 2, 1) + pltpu.roll(centre, lanes - 2, 1)
        kinetic = 0.5 * (7.5 * centre - FOUR_THIRDS * near_sum + TWELFTH * far_sum)
        return kinetic + wide_pot[plane] * centre, centre

    def sweep(field, older, out, lo, hi, scale, carry_scale):
        for plane in range(lo, hi):
            for band in range(band_count):
                applied, centre = apply(field, band, plane)
                value = (applied - CENTER * centre) * scale
                if older is not None:
                    value = value - carry_scale * older[band, plane]
                out[band, plane] = value

    total = first_buf.shape[1]
    sweep(first_buf, None, second_buf, 2, total - 2, SIGMA_ONE / HALF_WIDTH, 0.0)
    bufs = [first_buf, second_buf, third_buf]
    older, field, spare = 0, 1, 2
    sigma_now = SIGMA_ONE
    for repeat_index in range(filter_degree - 1):
        sigma_next = 1.0 / (2.0 / SIGMA_ONE - sigma_now)
        margin = 2 * (repeat_index + 2)
        sweep(bufs[field], bufs[older], bufs[spare], margin, total - margin,
              2.0 * sigma_next / HALF_WIDTH, sigma_now * sigma_next)
        older, field, spare = field, spare, older
        sigma_now = sigma_next
    final = bufs[field]
    filtered_ref[...] = final[:, width : width + own_planes]

    for plane in range(width, width + own_planes):
        for band in range(band_count):
            image_ref[band, plane - width], _ = apply(final, band, plane)


def filter_and_image(below, own, above, below_pot, own_pot, above_pot):
    band_count = own.shape[0]
    own_planes, rows, lanes = own.shape[1], own.shape[2], own.shape[3]
    total = below.shape[1] + own_planes + above.shape[1]
    shape = (band_count, own_planes, rows, lanes)
    cells = band_count * total * rows * lanes
    return pl.pallas_call(
        filter_kernel,
        out_shape=(jax.ShapeDtypeStruct(shape, jnp.float32), jax.ShapeDtypeStruct(shape, jnp.float32)),
        in_specs=[pl.BlockSpec(memory_space=pltpu.VMEM)] * 6,
        out_specs=(pl.BlockSpec(memory_space=pltpu.VMEM), pl.BlockSpec(memory_space=pltpu.VMEM)),
        scratch_shapes=[pltpu.VMEM((band_count, total, rows, lanes), jnp.float32)] * 3
        + [pltpu.VMEM((total, rows, lanes), jnp.float32)],
        cost_estimate=pl.CostEstimate(flops=30 * cells * 4, transcendentals=0, bytes_accessed=4 * cells * 3),
    )(below, own, above, below_pot, own_pot, above_pot)


def replica_pairs(direction):
    grid_count, band_count = lax.axis_size("grid"), lax.axis_size("band")
    pairs = []
    for target_grid in range(grid_count):
        source_grid = (target_grid - direction) % grid_count
        far = source_grid // 8 != target_grid // 8
        for target_band in range(band_count):
            source_band = target_band ^ 4 if far else target_band
            pairs.append((source_band * grid_count + source_grid, target_band * grid_count + target_grid))
    return pairs


def on_device(trial_bands, potential):
    band_count = trial_bands.shape[0]
    width = 2 * (filter_degree + 1)
    count = lax.axis_size("grid")
    below = lax.ppermute(trial_bands[:, trial_bands.shape[1] - width :], "grid", [(i, (i + 1) % count) for i in range(count)])
    above = lax.ppermute(trial_bands[:, :width], "grid", [((i + 1) % count, i) for i in range(count)])
    below_pot = lax.ppermute(potential[potential.shape[0] - width :], ("band", "grid"), replica_pairs(1))
    above_pot = lax.ppermute(potential[:width], ("band", "grid"), replica_pairs(-1))
    current, applied = filter_and_image(below, trial_bands, above, below_pot, potential, above_pot)
    band_devices = lax.axis_size("band")
    total_bands = band_count * band_devices
    cell_count = current.shape[1] * current.shape[2] * current.shape[3]
    cell_total = cell_count * lax.axis_size("grid")
    inverse_cells = 1.0 / cell_total
    first_band = lax.axis_index("band") * band_count
    both = jnp.stack(
        [current.reshape(band_count, cell_count), applied.reshape(band_count, cell_count)]
    ).reshape(2, band_count, band_devices, cell_count // band_devices)
    moved = lax.all_to_all(both, "band", 2, 1, tiled=True)
    bands_here = moved[0].reshape(total_bands, -1)
    image_here = moved[1].reshape(total_bands, -1)
    margin_part = jnp.dot(
        bands_here, bands_here.T, precision=lax.Precision.HIGHEST, preferred_element_type=jnp.float32
    )
    image_part = jnp.dot(
        image_here, bands_here.T, precision=lax.Precision.HIGHEST, preferred_element_type=jnp.float32
    )
    norm_part = jnp.sum(image_here * image_here, axis=1)
    packed = jnp.concatenate([margin_part.reshape(-1), image_part.reshape(-1), norm_part])
    packed = butterfly_sum(packed, "grid", [flip(1), flip(2), ring_of_four(0, 2), flip(8)])
    packed = butterfly_sum(packed, "band", [flip(1), flip(2), flip(4), flip(8), ring_of_four(0, 8)])
    packed = packed * inverse_cells
    square = total_bands * total_bands
    margin = packed[:square].reshape(total_bands, total_bands)
    subspace = packed[square : 2 * square].reshape(total_bands, total_bands)
    image_norms = packed[2 * square :]
    factor = jnp.linalg.cholesky(margin)
    coefficients = lax.linalg.triangular_solve(factor, subspace.T, left_side=True, lower=True)
    projected = lax.linalg.triangular_solve(factor, coefficients.T, left_side=True, lower=True)
    residual_norms = image_norms - jnp.sum(coefficients * coefficients, axis=0)
    projected_rows = lax.dynamic_slice_in_dim(projected, first_band, band_count, 0)
    residual_rows = lax.dynamic_slice_in_dim(residual_norms, first_band, band_count, 0)
    return (current, projected_rows, residual_rows)


def solution(mesh):
    in_specs = (P("band", "grid", None, None), P("grid", None, None))
    out_specs = (P("band", "grid", None, None), P("band", None), P("band"))
    return jax.shard_map(
        on_device, mesh=mesh, in_specs=in_specs, out_specs=out_specs, check_vma=False
    )
```

```python
import jax
import jax.numpy as jnp
from jax import lax
from jax.experimental import pallas as pl
from jax.experimental.pallas import tpu as pltpu
from jax.sharding import PartitionSpec as P

CENTER = 4.25
HALF_WIDTH = 3.75
LOWEST = -2.0
SIGMA_ONE = HALF_WIDTH / (LOWEST - CENTER)
FOUR_THIRDS = 4.0 / 3.0
TWELFTH = 1.0 / 12.0
filter_degree = 4


def butterfly_sum(values, axis, partner_rounds):
    count = lax.axis_size(axis)
    for partner in partner_rounds:
        pairs = [(i, partner(i)) for i in range(count)]
        values = values + lax.ppermute(values, axis, pairs)
    return values


def flip(bit):
    return lambda i: i ^ bit


def ring_of_four(low, stride):
    def partner(i):
        place = (i // stride) % 4
        return i + (3 - 2 * place) * stride

    return partner


def filter_kernel(below_ref, own_ref, above_ref, below_pot, own_pot, above_pot, filtered_ref, image_ref,
                  first_buf, second_buf, third_buf, wide_pot):
    band_count, own_planes = filtered_ref.shape[0], filtered_ref.shape[1]
    width = below_ref.shape[1]
    for at, source, pot in ((0, below_ref, below_pot), (width, own_ref, own_pot),
                            (width + own_planes, above_ref, above_pot)):
        first_buf[:, at : at + source.shape[1]] = source[...]
        wide_pot[at : at + source.shape[1]] = pot[...]
    rows, lanes = first_buf.shape[2], first_buf.shape[3]

    def apply(field, band, plane):
        centre = field[band, plane]
        near_sum = field[band, plane - 1] + field[band, plane + 1]
        near_sum = near_sum + pltpu.roll(centre, 1, 0) + pltpu.roll(centre, rows - 1, 0)
        near_sum = near_sum + pltpu.roll(centre, 1, 1) + pltpu.roll(centre, lanes - 1, 1)
        far_sum = field[band, plane - 2] + field[band, plane + 2]
        far_sum = far_sum + pltpu.roll(centre, 2, 0) + pltpu.roll(centre, rows - 2, 0)
        far_sum = far_sum + pltpu.roll(centre, 2, 1) + pltpu.roll(centre, lanes - 2, 1)
        kinetic = 0.5 * (7.5 * centre - FOUR_THIRDS * near_sum + TWELFTH * far_sum)
        return kinetic + wide_pot[plane] * centre, centre

    def sweep(field, older, out, lo, hi, scale, carry_scale):
        for plane in range(lo, hi):
            for band in range(band_count):
                applied, centre = apply(field, band, plane)
                value = (applied - CENTER * centre) * scale
                if older is not None:
                    value = value - carry_scale * older[band, plane]
                out[band, plane] = value

    total = first_buf.shape[1]
    sweep(first_buf, None, second_buf, 2, total - 2, SIGMA_ONE / HALF_WIDTH, 0.0)
    bufs = [first_buf, second_buf, third_buf]
    older, field, spare = 0, 1, 2
    sigma_now = SIGMA_ONE
    for repeat_index in range(filter_degree - 1):
        sigma_next = 1.0 / (2.0 / SIGMA_ONE - sigma_now)
        margin = 2 * (repeat_index + 2)
        sweep(bufs[field], bufs[older], bufs[spare], margin, total - margin,
              2.0 * sigma_next / HALF_WIDTH, sigma_now * sigma_next)
        older, field, spare = field, spare, older
        sigma_now = sigma_next
    final = bufs[field]
    filtered_ref[...] = final[:, width : width + own_planes]

    for plane in range(width, width + own_planes):
        for band in range(band_count):
            image_ref[band, plane - width], _ = apply(final, band, plane)


def filter_and_image(below, own, above, below_pot, own_pot, above_pot):
    band_count = own.shape[0]
    own_planes, rows, lanes = own.shape[1], own.shape[2], own.shape[3]
    total = below.shape[1] + own_planes + above.shape[1]
    shape = (band_count, own_planes, rows, lanes)
    cells = band_count * total * rows * lanes
    return pl.pallas_call(
        filter_kernel,
        out_shape=(jax.ShapeDtypeStruct(shape, jnp.float32), jax.ShapeDtypeStruct(shape, jnp.float32)),
        in_specs=[pl.BlockSpec(memory_space=pltpu.VMEM)] * 6,
        out_specs=(pl.BlockSpec(memory_space=pltpu.VMEM), pl.BlockSpec(memory_space=pltpu.VMEM)),
        scratch_shapes=[pltpu.VMEM((band_count, total, rows, lanes), jnp.float32)] * 3
        + [pltpu.VMEM((total, rows, lanes), jnp.float32)],
        cost_estimate=pl.CostEstimate(flops=30 * cells * 4, transcendentals=0, bytes_accessed=4 * cells * 3),
    )(below, own, above, below_pot, own_pot, above_pot)


def rayleigh_ritz_kernel(margin_ref, subspace_ref, norms_ref, projected_ref, residual_ref):
    size = margin_ref.shape[0]
    work = margin_ref[...]
    rows = lax.broadcasted_iota(jnp.int32, (size, size), 0)
    cols = lax.broadcasted_iota(jnp.int32, (size, size), 1)
    row_index = rows[:, :1]
    col_index = cols[:1, :]
    factor = jnp.zeros((size, size), jnp.float32)
    factor_t = jnp.zeros((size, size), jnp.float32)
    pivots = []
    for k in range(size):
        root = jnp.sqrt(work[k : k + 1, k : k + 1])
        column = jnp.where(row_index >= k, work[:, k : k + 1] / root, 0.0)
        row = jnp.where(col_index >= k, work[k : k + 1, :] / root, 0.0)
        work = work - column * row
        factor = jnp.where(cols == k, column, factor)
        factor_t = jnp.where(rows == k, row, factor_t)
        pivots.append(root)
    rest = subspace_ref[...]
    coeff_t = jnp.zeros((size, size), jnp.float32)
    for j in range(size):
        column = rest[:, j : j + 1] / pivots[j]
        rest = rest - column * jnp.where(col_index > j, factor_t[j : j + 1, :], 0.0)
        coeff_t = jnp.where(cols == j, column, coeff_t)
    rest = coeff_t
    projected = jnp.zeros((size, size), jnp.float32)
    for i in range(size):
        row = rest[i : i + 1, :] / pivots[i]
        rest = rest - jnp.where(row_index > i, factor[:, i : i + 1], 0.0) * row
        projected = jnp.where(rows == i, row, projected)
    projected_ref[...] = projected
    residual_ref[...] = norms_ref[...] - jnp.sum(coeff_t * coeff_t, axis=1, keepdims=True)


def rayleigh_ritz(margin, subspace, image_norms):
    size = margin.shape[0]
    return pl.pallas_call(
        rayleigh_ritz_kernel,
        out_shape=(jax.ShapeDtypeStruct((size, size), jnp.float32), jax.ShapeDtypeStruct((size, 1), jnp.float32)),
        in_specs=[pl.BlockSpec(memory_space=pltpu.VMEM)] * 3,
        out_specs=(pl.BlockSpec(memory_space=pltpu.VMEM), pl.BlockSpec(memory_space=pltpu.VMEM)),
        cost_estimate=pl.CostEstimate(flops=6 * size**3, transcendentals=size, bytes_accessed=4 * 4 * size * size),
    )(margin, subspace, image_norms.reshape(size, 1))


def replica_pairs(direction):
    grid_count, band_count = lax.axis_size("grid"), lax.axis_size("band")
    pairs = []
    for target_grid in range(grid_count):
        source_grid = (target_grid - direction) % grid_count
        far = source_grid // 8 != target_grid // 8
        for target_band in range(band_count):
            source_band = target_band ^ 4 if far else target_band
            pairs.append((source_band * grid_count + source_grid, target_band * grid_count + target_grid))
    return pairs


def on_device(trial_bands, potential):
    band_count = trial_bands.shape[0]
    width = 2 * (filter_degree + 1)
    count = lax.axis_size("grid")
    below = lax.ppermute(trial_bands[:, trial_bands.shape[1] - width :], "grid", [(i, (i + 1) % count) for i in range(count)])
    above = lax.ppermute(trial_bands[:, :width], "grid", [((i + 1) % count, i) for i in range(count)])
    below_pot = lax.ppermute(potential[potential.shape[0] - width :], ("band", "grid"), replica_pairs(1))
    above_pot = lax.ppermute(potential[:width], ("band", "grid"), replica_pairs(-1))
    current, applied = filter_and_image(below, trial_bands, above, below_pot, potential, above_pot)
    band_devices = lax.axis_size("band")
    total_bands = band_count * band_devices
    cell_count = current.shape[1] * current.shape[2] * current.shape[3]
    cell_total = cell_count * lax.axis_size("grid")
    inverse_cells = 1.0 / cell_total
    first_band = lax.axis_index("band") * band_count
    both = jnp.stack(
        [current.reshape(band_count, cell_count), applied.reshape(band_count, cell_count)]
    ).reshape(2, band_count, band_devices, cell_count // band_devices)
    moved = lax.all_to_all(both, "band", 2, 1, tiled=True)
    bands_here = moved[0].reshape(total_bands, -1)
    image_here = moved[1].reshape(total_bands, -1)
    margin_part = jnp.dot(
        bands_here, bands_here.T, precision=lax.Precision.HIGHEST, preferred_element_type=jnp.float32
    )
    image_part = jnp.dot(
        image_here, bands_here.T, precision=lax.Precision.HIGHEST, preferred_element_type=jnp.float32
    )
    norm_part = jnp.sum(image_here * image_here, axis=1)
    packed = jnp.concatenate([margin_part.reshape(-1), image_part.reshape(-1), norm_part])
    packed = butterfly_sum(packed, "grid", [flip(1), flip(2), ring_of_four(0, 2), flip(8)])
    packed = butterfly_sum(packed, "band", [flip(1), flip(2), flip(4), flip(8), ring_of_four(0, 8)])
    packed = packed * inverse_cells
    square = total_bands * total_bands
    margin = packed[:square].reshape(total_bands, total_bands)
    subspace = packed[square : 2 * square].reshape(total_bands, total_bands)
    image_norms = packed[2 * square :]
    margin = (margin + margin.T) / 2
    projected, residual_norms = rayleigh_ritz(margin, subspace, image_norms)
    residual_norms = residual_norms.reshape(-1)
    projected_rows = lax.dynamic_slice_in_dim(projected, first_band, band_count, 0)
    residual_rows = lax.dynamic_slice_in_dim(residual_norms, first_band, band_count, 0)
    return (current, projected_rows, residual_rows)


def solution(mesh):
    in_specs = (P("band", "grid", None, None), P("grid", None, None))
    out_specs = (P("band", "grid", None, None), P("band", None), P("band"))
    return jax.shard_map(
        on_device, mesh=mesh, in_specs=in_specs, out_specs=out_specs, check_vma=False
    )
```

```python
import jax
import jax.numpy as jnp
from jax import lax
from jax.experimental import pallas as pl
from jax.experimental.pallas import tpu as pltpu
from jax.sharding import PartitionSpec as P

CENTER = 4.25
HALF_WIDTH = 3.75
LOWEST = -2.0
SIGMA_ONE = HALF_WIDTH / (LOWEST - CENTER)
FOUR_THIRDS = 4.0 / 3.0
TWELFTH = 1.0 / 12.0
filter_degree = 4


def butterfly_sum(values, axis, partner_rounds):
    count = lax.axis_size(axis)
    for partner in partner_rounds:
        pairs = [(i, partner(i)) for i in range(count)]
        values = values + lax.ppermute(values, axis, pairs)
    return values


def flip(bit):
    return lambda i: i ^ bit


def ring_of_four(low, stride):
    def partner(i):
        place = (i // stride) % 4
        return i + (3 - 2 * place) * stride

    return partner


def filter_kernel(below_ref, own_ref, above_ref, below_pot, own_pot, above_pot, filtered_ref, image_ref,
                  first_buf, second_buf, third_buf, wide_pot):
    band_count, own_planes = filtered_ref.shape[0], filtered_ref.shape[1]
    width = below_ref.shape[1]
    for at, source, pot in ((0, below_ref, below_pot), (width, own_ref, own_pot),
                            (width + own_planes, above_ref, above_pot)):
        first_buf[:, at : at + source.shape[1]] = source[...]
        wide_pot[at : at + source.shape[1]] = pot[...]
    rows, lanes = first_buf.shape[2], first_buf.shape[3]

    def apply(field, band, plane):
        centre = field[band, plane]
        near_sum = field[band, plane - 1] + field[band, plane + 1]
        near_sum = near_sum + pltpu.roll(centre, 1, 0) + pltpu.roll(centre, rows - 1, 0)
        near_sum = near_sum + pltpu.roll(centre, 1, 1) + pltpu.roll(centre, lanes - 1, 1)
        far_sum = field[band, plane - 2] + field[band, plane + 2]
        far_sum = far_sum + pltpu.roll(centre, 2, 0) + pltpu.roll(centre, rows - 2, 0)
        far_sum = far_sum + pltpu.roll(centre, 2, 1) + pltpu.roll(centre, lanes - 2, 1)
        kinetic = 0.5 * (7.5 * centre - FOUR_THIRDS * near_sum + TWELFTH * far_sum)
        return kinetic + wide_pot[plane] * centre, centre

    def sweep(field, older, out, lo, hi, scale, carry_scale):
        for plane in range(lo, hi):
            for band in range(band_count):
                applied, centre = apply(field, band, plane)
                value = (applied - CENTER * centre) * scale
                if older is not None:
                    value = value - carry_scale * older[band, plane]
                out[band, plane] = value

    total = first_buf.shape[1]
    sweep(first_buf, None, second_buf, 2, total - 2, SIGMA_ONE / HALF_WIDTH, 0.0)
    bufs = [first_buf, second_buf, third_buf]
    older, field, spare = 0, 1, 2
    sigma_now = SIGMA_ONE
    for repeat_index in range(filter_degree - 1):
        sigma_next = 1.0 / (2.0 / SIGMA_ONE - sigma_now)
        margin = 2 * (repeat_index + 2)
        sweep(bufs[field], bufs[older], bufs[spare], margin, total - margin,
              2.0 * sigma_next / HALF_WIDTH, sigma_now * sigma_next)
        older, field, spare = field, spare, older
        sigma_now = sigma_next
    final = bufs[field]
    filtered_ref[...] = final[:, width : width + own_planes]

    for plane in range(width, width + own_planes):
        for band in range(band_count):
            image_ref[band, plane - width], _ = apply(final, band, plane)


def filter_and_image(below, own, above, below_pot, own_pot, above_pot):
    band_count = own.shape[0]
    own_planes, rows, lanes = own.shape[1], own.shape[2], own.shape[3]
    total = below.shape[1] + own_planes + above.shape[1]
    shape = (band_count, own_planes, rows, lanes)
    cells = band_count * total * rows * lanes
    return pl.pallas_call(
        filter_kernel,
        out_shape=(jax.ShapeDtypeStruct(shape, jnp.float32), jax.ShapeDtypeStruct(shape, jnp.float32)),
        in_specs=[pl.BlockSpec(memory_space=pltpu.VMEM)] * 6,
        out_specs=(pl.BlockSpec(memory_space=pltpu.VMEM), pl.BlockSpec(memory_space=pltpu.VMEM)),
        scratch_shapes=[pltpu.VMEM((band_count, total, rows, lanes), jnp.float32)] * 3
        + [pltpu.VMEM((total, rows, lanes), jnp.float32)],
        cost_estimate=pl.CostEstimate(flops=30 * cells * 4, transcendentals=0, bytes_accessed=4 * cells * 3),
    )(below, own, above, below_pot, own_pot, above_pot)


def rayleigh_ritz_kernel(first_ref, margin_ref, subspace_ref, norms_ref, projected_ref, residual_ref,
                         projected_buf, residual_buf):
    size = margin_ref.shape[0]
    work = margin_ref[...]
    rest = subspace_ref[...]
    rows = lax.broadcasted_iota(jnp.int32, (size, size), 0)
    cols = lax.broadcasted_iota(jnp.int32, (size, size), 1)
    row_index = rows[:, :1]
    col_index = cols[:1, :]
    coeff_t = jnp.zeros((size, size), jnp.float32)
    columns, inverses = [], []
    for k in range(size):
        inverse = 1.0 / jnp.sqrt(work[k : k + 1, k : k + 1])
        column = jnp.where(row_index >= k, work[:, k : k + 1] * inverse, 0.0)
        row = jnp.where(col_index >= k, work[k : k + 1, :] * inverse, 0.0)
        work = work - column * row
        solved = rest[:, k : k + 1] * inverse
        rest = rest - solved * jnp.where(col_index > k, row, 0.0)
        coeff_t = jnp.where(cols == k, solved, coeff_t)
        columns.append(jnp.where(row_index > k, column, 0.0))
        inverses.append(inverse)
    rest = coeff_t
    projected = jnp.zeros((size, size), jnp.float32)
    for i in range(size):
        row = rest[i : i + 1, :] * inverses[i]
        rest = rest - columns[i] * row
        projected = jnp.where(rows == i, row, projected)
    projected_buf[...] = projected
    residual_buf[...] = norms_ref[...] - jnp.sum(coeff_t * coeff_t, axis=1, keepdims=True)
    first = first_ref[0]
    count = projected_ref.shape[0]
    projected_ref[...] = projected_buf[pl.ds(first, count), :]
    residual_ref[...] = residual_buf[pl.ds(first, count), :]


def rayleigh_ritz(first_band, band_count, margin, subspace, image_norms):
    size = margin.shape[0]
    return pl.pallas_call(
        rayleigh_ritz_kernel,
        out_shape=(jax.ShapeDtypeStruct((band_count, size), jnp.float32),
                   jax.ShapeDtypeStruct((band_count, 1), jnp.float32)),
        in_specs=[pl.BlockSpec(memory_space=pltpu.SMEM)] + [pl.BlockSpec(memory_space=pltpu.VMEM)] * 3,
        out_specs=(pl.BlockSpec(memory_space=pltpu.VMEM), pl.BlockSpec(memory_space=pltpu.VMEM)),
        scratch_shapes=[pltpu.VMEM((size, size), jnp.float32), pltpu.VMEM((size, 1), jnp.float32)],
        cost_estimate=pl.CostEstimate(flops=6 * size**3, transcendentals=size, bytes_accessed=4 * 4 * size * size),
    )(first_band.reshape(1).astype(jnp.int32), margin, subspace, image_norms.reshape(size, 1))


def replica_pairs(direction):
    grid_count, band_count = lax.axis_size("grid"), lax.axis_size("band")
    pairs = []
    for target_grid in range(grid_count):
        source_grid = (target_grid - direction) % grid_count
        far = source_grid // 8 != target_grid // 8
        for target_band in range(band_count):
            source_band = target_band ^ 4 if far else target_band
            pairs.append((source_band * grid_count + source_grid, target_band * grid_count + target_grid))
    return pairs


def on_device(trial_bands, potential):
    band_count = trial_bands.shape[0]
    width = 2 * (filter_degree + 1)
    count = lax.axis_size("grid")
    below = lax.ppermute(trial_bands[:, trial_bands.shape[1] - width :], "grid", [(i, (i + 1) % count) for i in range(count)])
    above = lax.ppermute(trial_bands[:, :width], "grid", [((i + 1) % count, i) for i in range(count)])
    below_pot = lax.ppermute(potential[potential.shape[0] - width :], ("band", "grid"), replica_pairs(1))
    above_pot = lax.ppermute(potential[:width], ("band", "grid"), replica_pairs(-1))
    current, applied = filter_and_image(below, trial_bands, above, below_pot, potential, above_pot)
    band_devices = lax.axis_size("band")
    total_bands = band_count * band_devices
    cell_count = current.shape[1] * current.shape[2] * current.shape[3]
    cell_total = cell_count * lax.axis_size("grid")
    inverse_cells = 1.0 / cell_total
    first_band = lax.axis_index("band") * band_count
    both = jnp.stack(
        [current.reshape(band_count, cell_count), applied.reshape(band_count, cell_count)]
    ).reshape(2, band_count, band_devices, cell_count // band_devices)
    moved = lax.all_to_all(both, "band", 2, 1, tiled=True)
    bands_here = moved[0].reshape(total_bands, -1)
    image_here = moved[1].reshape(total_bands, -1)
    margin_part = jnp.dot(
        bands_here, bands_here.T, precision=lax.Precision.HIGHEST, preferred_element_type=jnp.float32
    )
    image_part = jnp.dot(
        image_here, bands_here.T, precision=lax.Precision.HIGHEST, preferred_element_type=jnp.float32
    )
    norm_part = jnp.sum(image_here * image_here, axis=1)
    packed = jnp.concatenate([margin_part.reshape(-1), image_part.reshape(-1), norm_part])
    packed = butterfly_sum(packed, "grid", [flip(1), flip(2), ring_of_four(0, 2), flip(8)])
    packed = butterfly_sum(packed, "band", [flip(1), flip(2), flip(4), flip(8), ring_of_four(0, 8)])
    packed = packed * inverse_cells
    square = total_bands * total_bands
    margin = packed[:square].reshape(total_bands, total_bands)
    subspace = packed[square : 2 * square].reshape(total_bands, total_bands)
    image_norms = packed[2 * square :]
    margin = (margin + margin.T) / 2
    projected_rows, residual_rows = rayleigh_ritz(first_band, band_count, margin, subspace, image_norms)
    residual_rows = residual_rows.reshape(-1)
    return (current, projected_rows, residual_rows)


def solution(mesh):
    in_specs = (P("band", "grid", None, None), P("grid", None, None))
    out_specs = (P("band", "grid", None, None), P("band", None), P("band"))
    return jax.shard_map(
        on_device, mesh=mesh, in_specs=in_specs, out_specs=out_specs, check_vma=False
    )
```

```python
import functools

import jax
import jax.numpy as jnp
from jax import lax
from jax.experimental import pallas as pl
from jax.experimental.pallas import tpu as pltpu
from jax.sharding import PartitionSpec as P

CENTER = 4.25
HALF_WIDTH = 3.75
LOWEST = -2.0
SIGMA_ONE = HALF_WIDTH / (LOWEST - CENTER)
FOUR_THIRDS = 4.0 / 3.0
TWELFTH = 1.0 / 12.0
filter_degree = 4


def butterfly_sum(values, axis, partner_rounds):
    count = lax.axis_size(axis)
    for partner in partner_rounds:
        pairs = [(i, partner(i)) for i in range(count)]
        values = values + lax.ppermute(values, axis, pairs)
    return values


def flip(bit):
    return lambda i: i ^ bit


def ring_of_four(low, stride):
    def partner(i):
        place = (i // stride) % 4
        return i + (3 - 2 * place) * stride

    return partner


def filter_kernel(below_ref, own_ref, above_ref, below_pot, own_pot, above_pot, filtered_ref, image_ref,
                  first_buf, second_buf, third_buf, wide_pot):
    band_count, own_planes = filtered_ref.shape[0], filtered_ref.shape[1]
    width = below_ref.shape[1]
    for at, source, pot in ((0, below_ref, below_pot), (width, own_ref, own_pot),
                            (width + own_planes, above_ref, above_pot)):
        first_buf[:, at : at + source.shape[1]] = source[...]
        wide_pot[at : at + source.shape[1]] = pot[...]
    rows, lanes = first_buf.shape[2], first_buf.shape[3]

    def apply(field, band, plane):
        centre = field[band, plane]
        near_sum = field[band, plane - 1] + field[band, plane + 1]
        near_sum = near_sum + pltpu.roll(centre, 1, 0) + pltpu.roll(centre, rows - 1, 0)
        near_sum = near_sum + pltpu.roll(centre, 1, 1) + pltpu.roll(centre, lanes - 1, 1)
        far_sum = field[band, plane - 2] + field[band, plane + 2]
        far_sum = far_sum + pltpu.roll(centre, 2, 0) + pltpu.roll(centre, rows - 2, 0)
        far_sum = far_sum + pltpu.roll(centre, 2, 1) + pltpu.roll(centre, lanes - 2, 1)
        kinetic = 0.5 * (7.5 * centre - FOUR_THIRDS * near_sum + TWELFTH * far_sum)
        return kinetic + wide_pot[plane] * centre, centre

    def sweep(field, older, out, lo, hi, scale, carry_scale):
        for plane in range(lo, hi):
            for band in range(band_count):
                applied, centre = apply(field, band, plane)
                value = (applied - CENTER * centre) * scale
                if older is not None:
                    value = value - carry_scale * older[band, plane]
                out[band, plane] = value

    total = first_buf.shape[1]
    sweep(first_buf, None, second_buf, 2, total - 2, SIGMA_ONE / HALF_WIDTH, 0.0)
    bufs = [first_buf, second_buf, third_buf]
    older, field, spare = 0, 1, 2
    sigma_now = SIGMA_ONE
    for repeat_index in range(filter_degree - 1):
        sigma_next = 1.0 / (2.0 / SIGMA_ONE - sigma_now)
        margin = 2 * (repeat_index + 2)
        sweep(bufs[field], bufs[older], bufs[spare], margin, total - margin,
              2.0 * sigma_next / HALF_WIDTH, sigma_now * sigma_next)
        older, field, spare = field, spare, older
        sigma_now = sigma_next
    final = bufs[field]
    filtered_ref[...] = final[:, width : width + own_planes]

    for plane in range(width, width + own_planes):
        for band in range(band_count):
            image_ref[band, plane - width], _ = apply(final, band, plane)


def filter_and_image(below, own, above, below_pot, own_pot, above_pot):
    band_count = own.shape[0]
    own_planes, rows, lanes = own.shape[1], own.shape[2], own.shape[3]
    total = below.shape[1] + own_planes + above.shape[1]
    shape = (band_count, own_planes, rows, lanes)
    cells = band_count * total * rows * lanes
    return pl.pallas_call(
        filter_kernel,
        out_shape=(jax.ShapeDtypeStruct(shape, jnp.float32), jax.ShapeDtypeStruct(shape, jnp.float32)),
        in_specs=[pl.BlockSpec(memory_space=pltpu.VMEM)] * 6,
        out_specs=(pl.BlockSpec(memory_space=pltpu.VMEM), pl.BlockSpec(memory_space=pltpu.VMEM)),
        scratch_shapes=[pltpu.VMEM((band_count, total, rows, lanes), jnp.float32)] * 3
        + [pltpu.VMEM((total, rows, lanes), jnp.float32)],
        cost_estimate=pl.CostEstimate(flops=30 * cells * 4, transcendentals=0, bytes_accessed=4 * cells * 3),
    )(below, own, above, below_pot, own_pot, above_pot)


def rayleigh_ritz_kernel(scale, first_ref, packed_ref, projected_ref, residual_ref, projected_buf, residual_buf):
    size = packed_ref.shape[0]
    work = packed_ref[:, 0:size] * scale
    rest = packed_ref[:, size : 2 * size] * scale
    norms = packed_ref[:, 2 * size : 2 * size + 1] * scale
    rows = lax.broadcasted_iota(jnp.int32, (size, size), 0)
    cols = lax.broadcasted_iota(jnp.int32, (size, size), 1)
    row_index = rows[:, :1]
    col_index = cols[:1, :]
    coeff_t = jnp.zeros((size, size), jnp.float32)
    columns, inverses = [], []
    for k in range(size):
        inverse = 1.0 / jnp.sqrt(work[k : k + 1, k : k + 1])
        column = jnp.where(row_index >= k, work[:, k : k + 1] * inverse, 0.0)
        row = jnp.where(col_index >= k, work[k : k + 1, :] * inverse, 0.0)
        work = work - column * row
        solved = rest[:, k : k + 1] * inverse
        rest = rest - solved * jnp.where(col_index > k, row, 0.0)
        coeff_t = jnp.where(cols == k, solved, coeff_t)
        columns.append(jnp.where(row_index > k, column, 0.0))
        inverses.append(inverse)
    rest = coeff_t
    projected = jnp.zeros((size, size), jnp.float32)
    for i in range(size):
        row = rest[i : i + 1, :] * inverses[i]
        rest = rest - columns[i] * row
        projected = jnp.where(rows == i, row, projected)
    projected_buf[...] = projected
    residual_buf[...] = norms - jnp.sum(coeff_t * coeff_t, axis=1, keepdims=True)
    first = first_ref[0]
    count = projected_ref.shape[0]
    projected_ref[...] = projected_buf[pl.ds(first, count), :]
    residual_ref[...] = residual_buf[pl.ds(first, count), :]


def rayleigh_ritz(first_band, band_count, packed, scale):
    size = packed.shape[0]
    return pl.pallas_call(
        functools.partial(rayleigh_ritz_kernel, scale),
        out_shape=(jax.ShapeDtypeStruct((band_count, size), jnp.float32),
                   jax.ShapeDtypeStruct((band_count, 1), jnp.float32)),
        in_specs=[pl.BlockSpec(memory_space=pltpu.SMEM), pl.BlockSpec(memory_space=pltpu.VMEM)],
        out_specs=(pl.BlockSpec(memory_space=pltpu.VMEM), pl.BlockSpec(memory_space=pltpu.VMEM)),
        scratch_shapes=[pltpu.VMEM((size, size), jnp.float32), pltpu.VMEM((size, 1), jnp.float32)],
        cost_estimate=pl.CostEstimate(flops=6 * size**3, transcendentals=size, bytes_accessed=4 * 4 * size * size),
    )(first_band.reshape(1).astype(jnp.int32), packed)


def replica_pairs(direction):
    grid_count, band_count = lax.axis_size("grid"), lax.axis_size("band")
    pairs = []
    for target_grid in range(grid_count):
        source_grid = (target_grid - direction) % grid_count
        far = source_grid // 8 != target_grid // 8
        for target_band in range(band_count):
            source_band = target_band ^ 4 if far else target_band
            pairs.append((source_band * grid_count + source_grid, target_band * grid_count + target_grid))
    return pairs


def on_device(trial_bands, potential):
    band_count = trial_bands.shape[0]
    width = 2 * (filter_degree + 1)
    count = lax.axis_size("grid")
    below = lax.ppermute(trial_bands[:, trial_bands.shape[1] - width :], "grid", [(i, (i + 1) % count) for i in range(count)])
    above = lax.ppermute(trial_bands[:, :width], "grid", [((i + 1) % count, i) for i in range(count)])
    below_pot = lax.ppermute(potential[potential.shape[0] - width :], ("band", "grid"), replica_pairs(1))
    above_pot = lax.ppermute(potential[:width], ("band", "grid"), replica_pairs(-1))
    current, applied = filter_and_image(below, trial_bands, above, below_pot, potential, above_pot)
    band_devices = lax.axis_size("band")
    total_bands = band_count * band_devices
    cell_count = current.shape[1] * current.shape[2] * current.shape[3]
    cell_total = cell_count * lax.axis_size("grid")
    inverse_cells = 1.0 / cell_total
    first_band = lax.axis_index("band") * band_count
    both = jnp.stack(
        [current.reshape(band_count, cell_count), applied.reshape(band_count, cell_count)]
    ).reshape(2, band_count, band_devices, cell_count // band_devices)
    moved = lax.all_to_all(both, "band", 2, 1, tiled=True)
    bands_here = moved[0].reshape(total_bands, -1)
    image_here = moved[1].reshape(total_bands, -1)
    margin_part = jnp.dot(
        bands_here, bands_here.T, precision=lax.Precision.HIGHEST, preferred_element_type=jnp.float32
    )
    image_part = jnp.dot(
        image_here, bands_here.T, precision=lax.Precision.HIGHEST, preferred_element_type=jnp.float32
    )
    norm_part = jnp.sum(image_here * image_here, axis=1)
    margin_part = (margin_part + margin_part.T) / 2
    packed = jnp.concatenate([margin_part, image_part, norm_part[:, None]], axis=1)
    packed = butterfly_sum(packed, "grid", [flip(1), flip(2), ring_of_four(0, 2), flip(8)])
    packed = butterfly_sum(packed, "band", [flip(1), flip(2), flip(4), flip(8), ring_of_four(0, 8)])
    projected_rows, residual_rows = rayleigh_ritz(first_band, band_count, packed, inverse_cells)
    residual_rows = residual_rows.reshape(-1)
    return (current, projected_rows, residual_rows)


def solution(mesh):
    in_specs = (P("band", "grid", None, None), P("grid", None, None))
    out_specs = (P("band", "grid", None, None), P("band", None), P("band"))
    return jax.shard_map(
        on_device, mesh=mesh, in_specs=in_specs, out_specs=out_specs, check_vma=False
    )
```

```python
import jax
import jax.numpy as jnp
from jax import lax
from jax.experimental import pallas as pl
from jax.experimental.pallas import tpu as pltpu
from jax.sharding import PartitionSpec as P

CENTER = 4.25
HALF_WIDTH = 3.75
LOWEST = -2.0
SIGMA_ONE = HALF_WIDTH / (LOWEST - CENTER)
FOUR_THIRDS = 4.0 / 3.0
TWELFTH = 1.0 / 12.0
filter_degree = 4


def butterfly_sum(values, axis, partner_rounds):
    count = lax.axis_size(axis)
    for partner in partner_rounds:
        pairs = [(i, partner(i)) for i in range(count)]
        values = values + lax.ppermute(values, axis, pairs)
    return values


def flip(bit):
    return lambda i: i ^ bit


def ring_of_four(low, stride):
    def partner(i):
        place = (i // stride) % 4
        return i + (3 - 2 * place) * stride

    return partner


def filter_kernel(below_ref, own_ref, above_ref, below_pot, own_pot, above_pot, filtered_ref, image_ref,
                  first_buf, second_buf, third_buf, wide_pot):
    band_count, own_planes = filtered_ref.shape[0], filtered_ref.shape[1]
    width = below_ref.shape[1]
    for at, source, pot in ((0, below_ref, below_pot), (width, own_ref, own_pot),
                            (width + own_planes, above_ref, above_pot)):
        first_buf[:, at : at + source.shape[1]] = source[...]
        wide_pot[at : at + source.shape[1]] = pot[...]
    rows, lanes = first_buf.shape[2], first_buf.shape[3]

    def apply(field, band, plane):
        centre = field[band, plane]
        near_sum = field[band, plane - 1] + field[band, plane + 1]
        near_sum = near_sum + pltpu.roll(centre, 1, 0) + pltpu.roll(centre, rows - 1, 0)
        near_sum = near_sum + pltpu.roll(centre, 1, 1) + pltpu.roll(centre, lanes - 1, 1)
        far_sum = field[band, plane - 2] + field[band, plane + 2]
        far_sum = far_sum + pltpu.roll(centre, 2, 0) + pltpu.roll(centre, rows - 2, 0)
        far_sum = far_sum + pltpu.roll(centre, 2, 1) + pltpu.roll(centre, lanes - 2, 1)
        kinetic = 0.5 * (7.5 * centre - FOUR_THIRDS * near_sum + TWELFTH * far_sum)
        return kinetic + wide_pot[plane] * centre, centre

    def sweep(field, older, out, lo, hi, scale, carry_scale):
        for plane in range(lo, hi):
            for band in range(band_count):
                applied, centre = apply(field, band, plane)
                value = (applied - CENTER * centre) * scale
                if older is not None:
                    value = value - carry_scale * older[band, plane]
                out[band, plane] = value

    total = first_buf.shape[1]
    sweep(first_buf, None, second_buf, 2, total - 2, SIGMA_ONE / HALF_WIDTH, 0.0)
    bufs = [first_buf, second_buf, third_buf]
    older, field, spare = 0, 1, 2
    sigma_now = SIGMA_ONE
    for repeat_index in range(filter_degree - 1):
        sigma_next = 1.0 / (2.0 / SIGMA_ONE - sigma_now)
        margin = 2 * (repeat_index + 2)
        sweep(bufs[field], bufs[older], bufs[spare], margin, total - margin,
              2.0 * sigma_next / HALF_WIDTH, sigma_now * sigma_next)
        older, field, spare = field, spare, older
        sigma_now = sigma_next
    final = bufs[field]
    filtered_ref[...] = final[:, width : width + own_planes]

    for plane in range(width, width + own_planes):
        for band in range(band_count):
            image_ref[band, plane - width], _ = apply(final, band, plane)


def filter_and_image(below, own, above, below_pot, own_pot, above_pot):
    band_count = own.shape[0]
    own_planes, rows, lanes = own.shape[1], own.shape[2], own.shape[3]
    total = below.shape[1] + own_planes + above.shape[1]
    shape = (band_count, own_planes, rows, lanes)
    cells = band_count * total * rows * lanes
    return pl.pallas_call(
        filter_kernel,
        out_shape=(jax.ShapeDtypeStruct(shape, jnp.float32), jax.ShapeDtypeStruct(shape, jnp.float32)),
        in_specs=[pl.BlockSpec(memory_space=pltpu.VMEM)] * 6,
        out_specs=(pl.BlockSpec(memory_space=pltpu.VMEM), pl.BlockSpec(memory_space=pltpu.VMEM)),
        scratch_shapes=[pltpu.VMEM((band_count, total, rows, lanes), jnp.float32)] * 3
        + [pltpu.VMEM((total, rows, lanes), jnp.float32)],
        cost_estimate=pl.CostEstimate(flops=30 * cells * 4, transcendentals=0, bytes_accessed=4 * cells * 3),
    )(below, own, above, below_pot, own_pot, above_pot)


def rayleigh_ritz_kernel(first_ref, margin_ref, subspace_ref, norms_ref, projected_ref, residual_ref,
                         projected_buf, residual_buf):
    size = margin_ref.shape[0]
    work = margin_ref[...]
    rest = subspace_ref[...]
    rows = lax.broadcasted_iota(jnp.int32, (size, size), 0)
    cols = lax.broadcasted_iota(jnp.int32, (size, size), 1)
    row_index = rows[:, :1]
    col_index = cols[:1, :]
    coeff_t = jnp.zeros((size, size), jnp.float32)
    columns, inverses = [], []
    for k in range(size):
        inverse = 1.0 / jnp.sqrt(work[k : k + 1, k : k + 1])
        column = jnp.where(row_index >= k, work[:, k : k + 1] * inverse, 0.0)
        row = jnp.where(col_index >= k, work[k : k + 1, :] * inverse, 0.0)
        work = work - column * row
        solved = rest[:, k : k + 1] * inverse
        rest = rest - solved * jnp.where(col_index > k, row, 0.0)
        coeff_t = jnp.where(cols == k, solved, coeff_t)
        columns.append(jnp.where(row_index > k, column, 0.0))
        inverses.append(inverse)
    rest = coeff_t
    projected = jnp.zeros((size, size), jnp.float32)
    for i in range(size):
        row = rest[i : i + 1, :] * inverses[i]
        rest = rest - columns[i] * row
        projected = jnp.where(rows == i, row, projected)
    projected_buf[...] = projected
    residual_buf[...] = norms_ref[...] - jnp.sum(coeff_t * coeff_t, axis=1, keepdims=True)
    first = first_ref[0]
    count = projected_ref.shape[0]
    projected_ref[...] = projected_buf[pl.ds(first, count), :]
    residual_ref[...] = residual_buf[pl.ds(first, count), :]


def rayleigh_ritz(first_band, band_count, margin, subspace, image_norms):
    size = margin.shape[0]
    return pl.pallas_call(
        rayleigh_ritz_kernel,
        out_shape=(jax.ShapeDtypeStruct((band_count, size), jnp.float32),
                   jax.ShapeDtypeStruct((band_count, 1), jnp.float32)),
        in_specs=[pl.BlockSpec(memory_space=pltpu.SMEM)] + [pl.BlockSpec(memory_space=pltpu.VMEM)] * 3,
        out_specs=(pl.BlockSpec(memory_space=pltpu.VMEM), pl.BlockSpec(memory_space=pltpu.VMEM)),
        scratch_shapes=[pltpu.VMEM((size, size), jnp.float32), pltpu.VMEM((size, 1), jnp.float32)],
        cost_estimate=pl.CostEstimate(flops=6 * size**3, transcendentals=size, bytes_accessed=4 * 4 * size * size),
    )(first_band.reshape(1).astype(jnp.int32), margin, subspace, image_norms.reshape(size, 1))


def replica_pairs(direction):
    grid_count, band_count = lax.axis_size("grid"), lax.axis_size("band")
    pairs = []
    for target_grid in range(grid_count):
        source_grid = (target_grid - direction) % grid_count
        far = source_grid // 8 != target_grid // 8
        for target_band in range(band_count):
            source_band = target_band ^ 4 if far else target_band
            pairs.append((source_band * grid_count + source_grid, target_band * grid_count + target_grid))
    return pairs


def on_device(trial_bands, potential):
    band_count = trial_bands.shape[0]
    width = 2 * (filter_degree + 1)
    count = lax.axis_size("grid")
    below = lax.ppermute(trial_bands[:, trial_bands.shape[1] - width :], "grid", [(i, (i + 1) % count) for i in range(count)])
    above = lax.ppermute(trial_bands[:, :width], "grid", [((i + 1) % count, i) for i in range(count)])
    below_pot = lax.ppermute(potential[potential.shape[0] - width :], ("band", "grid"), replica_pairs(1))
    above_pot = lax.ppermute(potential[:width], ("band", "grid"), replica_pairs(-1))
    current, applied = filter_and_image(below, trial_bands, above, below_pot, potential, above_pot)
    band_devices = lax.axis_size("band")
    total_bands = band_count * band_devices
    cell_count = current.shape[1] * current.shape[2] * current.shape[3]
    cell_total = cell_count * lax.axis_size("grid")
    inverse_cells = 1.0 / cell_total
    first_band = lax.axis_index("band") * band_count
    both = jnp.stack(
        [current.reshape(band_count, cell_count), applied.reshape(band_count, cell_count)]
    ).reshape(2, band_count, band_devices, cell_count // band_devices)
    moved = lax.all_to_all(both, "band", 2, 1, tiled=True)
    bands_here = moved[0].reshape(total_bands, -1)
    image_here = moved[1].reshape(total_bands, -1)
    margin_part = jnp.dot(
        bands_here, bands_here.T, precision=lax.Precision.HIGHEST, preferred_element_type=jnp.float32
    )
    image_part = jnp.dot(
        image_here, bands_here.T, precision=lax.Precision.HIGHEST, preferred_element_type=jnp.float32
    )
    norm_part = jnp.sum(image_here * image_here, axis=1)
    packed = jnp.concatenate([margin_part.reshape(-1), image_part.reshape(-1), norm_part])
    packed = butterfly_sum(packed, "band", [flip(1), flip(2), flip(4), flip(8), ring_of_four(0, 8)])
    packed = butterfly_sum(packed, "grid", [flip(1), flip(2), ring_of_four(0, 2), flip(8)])
    packed = packed * inverse_cells
    square = total_bands * total_bands
    margin = packed[:square].reshape(total_bands, total_bands)
    subspace = packed[square : 2 * square].reshape(total_bands, total_bands)
    image_norms = packed[2 * square :]
    margin = (margin + margin.T) / 2
    projected_rows, residual_rows = rayleigh_ritz(first_band, band_count, margin, subspace, image_norms)
    residual_rows = residual_rows.reshape(-1)
    return (current, projected_rows, residual_rows)


def solution(mesh):
    in_specs = (P("band", "grid", None, None), P("grid", None, None))
    out_specs = (P("band", "grid", None, None), P("band", None), P("band"))
    return jax.shard_map(
        on_device, mesh=mesh, in_specs=in_specs, out_specs=out_specs, check_vma=False
    )
```

```python
import jax
import jax.numpy as jnp
from jax import lax
from jax.experimental import pallas as pl
from jax.experimental.pallas import tpu as pltpu
from jax.sharding import PartitionSpec as P

CENTER = 4.25
HALF_WIDTH = 3.75
LOWEST = -2.0
SIGMA_ONE = HALF_WIDTH / (LOWEST - CENTER)
FOUR_THIRDS = 4.0 / 3.0
TWELFTH = 1.0 / 12.0
filter_degree = 4


def butterfly_sum(values, axis, partner_rounds):
    count = lax.axis_size(axis)
    for partner in partner_rounds:
        pairs = [(i, partner(i)) for i in range(count)]
        values = values + lax.ppermute(values, axis, pairs)
    return values


def flip(bit):
    return lambda i: i ^ bit


def ring_of_four(low, stride):
    def partner(i):
        place = (i // stride) % 4
        return i + (3 - 2 * place) * stride

    return partner


def filter_kernel(below_ref, own_ref, above_ref, below_pot, own_pot, above_pot, filtered_ref, image_ref,
                  first_buf, second_buf, third_buf, wide_pot):
    band_count, own_planes = filtered_ref.shape[0], filtered_ref.shape[1]
    width = below_ref.shape[1]
    for at, source, pot in ((0, below_ref, below_pot), (width, own_ref, own_pot),
                            (width + own_planes, above_ref, above_pot)):
        first_buf[:, at : at + source.shape[1]] = source[...]
        wide_pot[at : at + source.shape[1]] = pot[...]
    rows, lanes = first_buf.shape[2], first_buf.shape[3]

    def apply(field, band, plane):
        centre = field[band, plane]
        near_sum = field[band, plane - 1] + field[band, plane + 1]
        near_sum = near_sum + pltpu.roll(centre, 1, 0) + pltpu.roll(centre, rows - 1, 0)
        near_sum = near_sum + pltpu.roll(centre, 1, 1) + pltpu.roll(centre, lanes - 1, 1)
        far_sum = field[band, plane - 2] + field[band, plane + 2]
        far_sum = far_sum + pltpu.roll(centre, 2, 0) + pltpu.roll(centre, rows - 2, 0)
        far_sum = far_sum + pltpu.roll(centre, 2, 1) + pltpu.roll(centre, lanes - 2, 1)
        kinetic = 0.5 * (7.5 * centre - FOUR_THIRDS * near_sum + TWELFTH * far_sum)
        return kinetic + wide_pot[plane] * centre, centre

    def sweep(field, older, out, lo, hi, scale, carry_scale):
        for plane in range(lo, hi):
            for band in range(band_count):
                applied, centre = apply(field, band, plane)
                value = (applied - CENTER * centre) * scale
                if older is not None:
                    value = value - carry_scale * older[band, plane]
                out[band, plane] = value

    total = first_buf.shape[1]
    sweep(first_buf, None, second_buf, 2, total - 2, SIGMA_ONE / HALF_WIDTH, 0.0)
    bufs = [first_buf, second_buf, third_buf]
    older, field, spare = 0, 1, 2
    sigma_now = SIGMA_ONE
    for repeat_index in range(filter_degree - 1):
        sigma_next = 1.0 / (2.0 / SIGMA_ONE - sigma_now)
        margin = 2 * (repeat_index + 2)
        sweep(bufs[field], bufs[older], bufs[spare], margin, total - margin,
              2.0 * sigma_next / HALF_WIDTH, sigma_now * sigma_next)
        older, field, spare = field, spare, older
        sigma_now = sigma_next
    final = bufs[field]
    filtered_ref[...] = final[:, width : width + own_planes]

    for plane in range(width, width + own_planes):
        for band in range(band_count):
            image_ref[band, plane - width], _ = apply(final, band, plane)


def filter_and_image(below, own, above, below_pot, own_pot, above_pot):
    band_count = own.shape[0]
    own_planes, rows, lanes = own.shape[1], own.shape[2], own.shape[3]
    total = below.shape[1] + own_planes + above.shape[1]
    shape = (band_count, own_planes, rows, lanes)
    cells = band_count * total * rows * lanes
    return pl.pallas_call(
        filter_kernel,
        out_shape=(jax.ShapeDtypeStruct(shape, jnp.float32), jax.ShapeDtypeStruct(shape, jnp.float32)),
        in_specs=[pl.BlockSpec(memory_space=pltpu.VMEM)] * 6,
        out_specs=(pl.BlockSpec(memory_space=pltpu.VMEM), pl.BlockSpec(memory_space=pltpu.VMEM)),
        scratch_shapes=[pltpu.VMEM((band_count, total, rows, lanes), jnp.float32)] * 3
        + [pltpu.VMEM((total, rows, lanes), jnp.float32)],
        cost_estimate=pl.CostEstimate(flops=30 * cells * 4, transcendentals=0, bytes_accessed=4 * cells * 3),
    )(below, own, above, below_pot, own_pot, above_pot)


def rayleigh_ritz_kernel(first_ref, margin_ref, subspace_ref, norms_ref, projected_ref, residual_ref,
                         projected_buf, residual_buf):
    size = margin_ref.shape[0]
    work = margin_ref[...]
    rest = subspace_ref[...]
    rows = lax.broadcasted_iota(jnp.int32, (size, size), 0)
    cols = lax.broadcasted_iota(jnp.int32, (size, size), 1)
    row_index = rows[:, :1]
    col_index = cols[:1, :]
    coeff_t = jnp.zeros((size, size), jnp.float32)
    columns, inverses = [], []
    for k in range(size):
        inverse = 1.0 / jnp.sqrt(work[k : k + 1, k : k + 1])
        column = jnp.where(row_index >= k, work[:, k : k + 1] * inverse, 0.0)
        row = jnp.where(col_index >= k, work[k : k + 1, :] * inverse, 0.0)
        work = work - column * row
        solved = rest[:, k : k + 1] * inverse
        rest = rest - solved * jnp.where(col_index > k, row, 0.0)
        coeff_t = jnp.where(cols == k, solved, coeff_t)
        columns.append(jnp.where(row_index > k, column, 0.0))
        inverses.append(inverse)
    rest = coeff_t
    projected = jnp.zeros((size, size), jnp.float32)
    for i in range(size):
        row = rest[i : i + 1, :] * inverses[i]
        rest = rest - columns[i] * row
        projected = jnp.where(rows == i, row, projected)
    projected_buf[...] = projected
    residual_buf[...] = norms_ref[...] - jnp.sum(coeff_t * coeff_t, axis=1, keepdims=True)
    first = first_ref[0]
    count = projected_ref.shape[0]
    projected_ref[...] = projected_buf[pl.ds(first, count), :]
    residual_ref[...] = residual_buf[pl.ds(first, count), :]


def rayleigh_ritz(first_band, band_count, margin, subspace, image_norms):
    size = margin.shape[0]
    return pl.pallas_call(
        rayleigh_ritz_kernel,
        out_shape=(jax.ShapeDtypeStruct((band_count, size), jnp.float32),
                   jax.ShapeDtypeStruct((band_count, 1), jnp.float32)),
        in_specs=[pl.BlockSpec(memory_space=pltpu.SMEM)] + [pl.BlockSpec(memory_space=pltpu.VMEM)] * 3,
        out_specs=(pl.BlockSpec(memory_space=pltpu.VMEM), pl.BlockSpec(memory_space=pltpu.VMEM)),
        scratch_shapes=[pltpu.VMEM((size, size), jnp.float32), pltpu.VMEM((size, 1), jnp.float32)],
        cost_estimate=pl.CostEstimate(flops=6 * size**3, transcendentals=size, bytes_accessed=4 * 4 * size * size),
    )(first_band.reshape(1).astype(jnp.int32), margin, subspace, image_norms.reshape(size, 1))


def replica_pairs(direction):
    grid_count, band_count = lax.axis_size("grid"), lax.axis_size("band")
    pairs = []
    for target_grid in range(grid_count):
        source_grid = (target_grid - direction) % grid_count
        far = source_grid // 8 != target_grid // 8
        for target_band in range(band_count):
            source_band = target_band ^ 4 if far else target_band
            pairs.append((source_band * grid_count + source_grid, target_band * grid_count + target_grid))
    return pairs


def on_device(trial_bands, potential):
    band_count = trial_bands.shape[0]
    width = 2 * (filter_degree + 1)
    count = lax.axis_size("grid")
    below = lax.ppermute(trial_bands[:, trial_bands.shape[1] - width :], "grid", [(i, (i + 1) % count) for i in range(count)])
    above = lax.ppermute(trial_bands[:, :width], "grid", [((i + 1) % count, i) for i in range(count)])
    below_pot = lax.ppermute(potential[potential.shape[0] - width :], ("band", "grid"), replica_pairs(1))
    above_pot = lax.ppermute(potential[:width], ("band", "grid"), replica_pairs(-1))
    current, applied = filter_and_image(below, trial_bands, above, below_pot, potential, above_pot)
    band_devices = lax.axis_size("band")
    total_bands = band_count * band_devices
    cell_count = current.shape[1] * current.shape[2] * current.shape[3]
    cell_total = cell_count * lax.axis_size("grid")
    inverse_cells = 1.0 / cell_total
    first_band = lax.axis_index("band") * band_count
    both = jnp.stack(
        [current.reshape(band_count, cell_count), applied.reshape(band_count, cell_count)]
    ).reshape(2, band_count, band_devices, cell_count // band_devices)
    moved = lax.all_to_all(both, "band", 2, 1, tiled=True)
    bands_here = moved[0].reshape(total_bands, -1)
    image_here = moved[1].reshape(total_bands, -1)
    margin_part = jnp.dot(
        bands_here, bands_here.T, precision=lax.Precision.HIGHEST, preferred_element_type=jnp.float32
    )
    image_part = jnp.dot(
        image_here, bands_here.T, precision=lax.Precision.HIGHEST, preferred_element_type=jnp.float32
    )
    norm_part = jnp.sum(image_here * image_here, axis=1)
    packed = jnp.concatenate([margin_part.reshape(-1), image_part.reshape(-1), norm_part])
    packed = butterfly_sum(packed, "band", [flip(1), flip(2), flip(4), flip(8), ring_of_four(0, 8)])
    packed = butterfly_sum(packed, "grid", [flip(8), flip(2), ring_of_four(0, 2), flip(1)])
    packed = packed * inverse_cells
    square = total_bands * total_bands
    margin = packed[:square].reshape(total_bands, total_bands)
    subspace = packed[square : 2 * square].reshape(total_bands, total_bands)
    image_norms = packed[2 * square :]
    margin = (margin + margin.T) / 2
    projected_rows, residual_rows = rayleigh_ritz(first_band, band_count, margin, subspace, image_norms)
    residual_rows = residual_rows.reshape(-1)
    return (current, projected_rows, residual_rows)


def solution(mesh):
    in_specs = (P("band", "grid", None, None), P("grid", None, None))
    out_specs = (P("band", "grid", None, None), P("band", None), P("band"))
    return jax.shard_map(
        on_device, mesh=mesh, in_specs=in_specs, out_specs=out_specs, check_vma=False
    )
```

```python
import functools

import jax
import jax.numpy as jnp
from jax import lax
from jax.experimental import pallas as pl
from jax.experimental.pallas import tpu as pltpu
from jax.sharding import PartitionSpec as P

CENTER = 4.25
HALF_WIDTH = 3.75
LOWEST = -2.0
SIGMA_ONE = HALF_WIDTH / (LOWEST - CENTER)
FOUR_THIRDS = 4.0 / 3.0
TWELFTH = 1.0 / 12.0
filter_degree = 4


def butterfly_sum(values, axis, partner_rounds):
    count = lax.axis_size(axis)
    for partner in partner_rounds:
        pairs = [(i, partner(i)) for i in range(count)]
        values = values + lax.ppermute(values, axis, pairs)
    return values


def flip(bit):
    return lambda i: i ^ bit


def ring_of_four(low, stride):
    def partner(i):
        place = (i // stride) % 4
        return i + (3 - 2 * place) * stride

    return partner


def filter_kernel(below_ref, own_ref, above_ref, below_pot, own_pot, above_pot, filtered_ref, image_ref,
                  first_buf, second_buf, third_buf, wide_pot):
    band_count, own_planes = filtered_ref.shape[0], filtered_ref.shape[1]
    width = below_ref.shape[1]
    for at, source, pot in ((0, below_ref, below_pot), (width, own_ref, own_pot),
                            (width + own_planes, above_ref, above_pot)):
        first_buf[:, at : at + source.shape[1]] = source[...]
        wide_pot[at : at + source.shape[1]] = pot[...]
    rows, lanes = first_buf.shape[2], first_buf.shape[3]

    def apply(field, band, plane):
        centre = field[band, plane]
        near_sum = field[band, plane - 1] + field[band, plane + 1]
        near_sum = near_sum + pltpu.roll(centre, 1, 0) + pltpu.roll(centre, rows - 1, 0)
        near_sum = near_sum + pltpu.roll(centre, 1, 1) + pltpu.roll(centre, lanes - 1, 1)
        far_sum = field[band, plane - 2] + field[band, plane + 2]
        far_sum = far_sum + pltpu.roll(centre, 2, 0) + pltpu.roll(centre, rows - 2, 0)
        far_sum = far_sum + pltpu.roll(centre, 2, 1) + pltpu.roll(centre, lanes - 2, 1)
        kinetic = 0.5 * (7.5 * centre - FOUR_THIRDS * near_sum + TWELFTH * far_sum)
        return kinetic + wide_pot[plane] * centre, centre

    def sweep(field, older, out, lo, hi, scale, carry_scale):
        for plane in range(lo, hi):
            for band in range(band_count):
                applied, centre = apply(field, band, plane)
                value = (applied - CENTER * centre) * scale
                if older is not None:
                    value = value - carry_scale * older[band, plane]
                out[band, plane] = value

    total = first_buf.shape[1]
    sweep(first_buf, None, second_buf, 2, total - 2, SIGMA_ONE / HALF_WIDTH, 0.0)
    bufs = [first_buf, second_buf, third_buf]
    older, field, spare = 0, 1, 2
    sigma_now = SIGMA_ONE
    for repeat_index in range(filter_degree - 1):
        sigma_next = 1.0 / (2.0 / SIGMA_ONE - sigma_now)
        margin = 2 * (repeat_index + 2)
        sweep(bufs[field], bufs[older], bufs[spare], margin, total - margin,
              2.0 * sigma_next / HALF_WIDTH, sigma_now * sigma_next)
        older, field, spare = field, spare, older
        sigma_now = sigma_next
    final = bufs[field]
    filtered_ref[...] = final[:, width : width + own_planes]

    for plane in range(width, width + own_planes):
        for band in range(band_count):
            image_ref[band, plane - width], _ = apply(final, band, plane)


def filter_and_image(below, own, above, below_pot, own_pot, above_pot):
    band_count = own.shape[0]
    own_planes, rows, lanes = own.shape[1], own.shape[2], own.shape[3]
    total = below.shape[1] + own_planes + above.shape[1]
    shape = (band_count, own_planes, rows, lanes)
    cells = band_count * total * rows * lanes
    return pl.pallas_call(
        filter_kernel,
        out_shape=(jax.ShapeDtypeStruct(shape, jnp.float32), jax.ShapeDtypeStruct(shape, jnp.float32)),
        in_specs=[pl.BlockSpec(memory_space=pltpu.VMEM)] * 6,
        out_specs=(pl.BlockSpec(memory_space=pltpu.VMEM), pl.BlockSpec(memory_space=pltpu.VMEM)),
        scratch_shapes=[pltpu.VMEM((band_count, total, rows, lanes), jnp.float32)] * 3
        + [pltpu.VMEM((total, rows, lanes), jnp.float32)],
        cost_estimate=pl.CostEstimate(flops=30 * cells * 4, transcendentals=0, bytes_accessed=4 * cells * 3),
    )(below, own, above, below_pot, own_pot, above_pot)


def rayleigh_ritz_kernel(scale, first_ref, packed_ref, projected_ref, residual_ref, projected_buf, residual_buf):
    size = packed_ref.shape[1]
    work = packed_ref[0:size, :] * scale
    rest = packed_ref[size : 2 * size, :] * scale
    rows = lax.broadcasted_iota(jnp.int32, (size, size), 0)
    cols = lax.broadcasted_iota(jnp.int32, (size, size), 1)
    row_index = rows[:, :1]
    col_index = cols[:1, :]
    coeff_t = jnp.zeros((size, size), jnp.float32)
    columns, inverses = [], []
    for k in range(size):
        inverse = 1.0 / jnp.sqrt(work[k : k + 1, k : k + 1])
        column = jnp.where(row_index >= k, work[:, k : k + 1] * inverse, 0.0)
        row = jnp.where(col_index >= k, work[k : k + 1, :] * inverse, 0.0)
        work = work - column * row
        solved = rest[:, k : k + 1] * inverse
        rest = rest - solved * jnp.where(col_index > k, row, 0.0)
        coeff_t = jnp.where(cols == k, solved, coeff_t)
        columns.append(jnp.where(row_index > k, column, 0.0))
        inverses.append(inverse)
    rest = coeff_t
    projected = jnp.zeros((size, size), jnp.float32)
    for i in range(size):
        row = rest[i : i + 1, :] * inverses[i]
        rest = rest - columns[i] * row
        projected = jnp.where(rows == i, row, projected)
    projected_buf[...] = projected
    norms = jnp.sum(jnp.where(rows == cols, packed_ref[2 * size : 2 * size + 1, :] * scale, 0.0), axis=1, keepdims=True)
    residual_buf[...] = norms - jnp.sum(coeff_t * coeff_t, axis=1, keepdims=True)
    first = first_ref[0]
    count = projected_ref.shape[0]
    projected_ref[...] = projected_buf[pl.ds(first, count), :]
    residual_ref[...] = residual_buf[pl.ds(first, count), :]


def rayleigh_ritz(first_band, band_count, packed, scale):
    size = packed.shape[1]
    return pl.pallas_call(
        functools.partial(rayleigh_ritz_kernel, scale),
        out_shape=(jax.ShapeDtypeStruct((band_count, size), jnp.float32),
                   jax.ShapeDtypeStruct((band_count, 1), jnp.float32)),
        in_specs=[pl.BlockSpec(memory_space=pltpu.SMEM), pl.BlockSpec(memory_space=pltpu.VMEM)],
        out_specs=(pl.BlockSpec(memory_space=pltpu.VMEM), pl.BlockSpec(memory_space=pltpu.VMEM)),
        scratch_shapes=[pltpu.VMEM((size, size), jnp.float32), pltpu.VMEM((size, 1), jnp.float32)],
        cost_estimate=pl.CostEstimate(flops=6 * size**3, transcendentals=size, bytes_accessed=4 * 4 * size * size),
    )(first_band.reshape(1).astype(jnp.int32), packed)


def replica_pairs(direction):
    grid_count, band_count = lax.axis_size("grid"), lax.axis_size("band")
    pairs = []
    for target_grid in range(grid_count):
        source_grid = (target_grid - direction) % grid_count
        far = source_grid // 8 != target_grid // 8
        for target_band in range(band_count):
            source_band = target_band ^ 4 if far else target_band
            pairs.append((source_band * grid_count + source_grid, target_band * grid_count + target_grid))
    return pairs


def on_device(trial_bands, potential):
    band_count = trial_bands.shape[0]
    width = 2 * (filter_degree + 1)
    count = lax.axis_size("grid")
    below = lax.ppermute(trial_bands[:, trial_bands.shape[1] - width :], "grid", [(i, (i + 1) % count) for i in range(count)])
    above = lax.ppermute(trial_bands[:, :width], "grid", [((i + 1) % count, i) for i in range(count)])
    below_pot = lax.ppermute(potential[potential.shape[0] - width :], ("band", "grid"), replica_pairs(1))
    above_pot = lax.ppermute(potential[:width], ("band", "grid"), replica_pairs(-1))
    current, applied = filter_and_image(below, trial_bands, above, below_pot, potential, above_pot)
    band_devices = lax.axis_size("band")
    total_bands = band_count * band_devices
    cell_count = current.shape[1] * current.shape[2] * current.shape[3]
    cell_total = cell_count * lax.axis_size("grid")
    inverse_cells = 1.0 / cell_total
    first_band = lax.axis_index("band") * band_count
    both = jnp.stack(
        [current.reshape(band_count, cell_count), applied.reshape(band_count, cell_count)]
    ).reshape(2, band_count, band_devices, cell_count // band_devices)
    moved = lax.all_to_all(both, "band", 2, 1, tiled=True)
    bands_here = moved[0].reshape(total_bands, -1)
    image_here = moved[1].reshape(total_bands, -1)
    margin_part = jnp.dot(
        bands_here, bands_here.T, precision=lax.Precision.HIGHEST, preferred_element_type=jnp.float32
    )
    image_part = jnp.dot(
        image_here, bands_here.T, precision=lax.Precision.HIGHEST, preferred_element_type=jnp.float32
    )
    norm_part = jnp.sum(image_here * image_here, axis=1)
    margin_part = (margin_part + margin_part.T) / 2
    packed = jnp.concatenate([margin_part, image_part, norm_part[None, :]], axis=0)
    packed = butterfly_sum(packed, "band", [flip(1), flip(2), flip(4), flip(8), ring_of_four(0, 8)])
    packed = butterfly_sum(packed, "grid", [flip(1), flip(2), ring_of_four(0, 2), flip(8)])
    projected_rows, residual_rows = rayleigh_ritz(first_band, band_count, packed, inverse_cells)
    residual_rows = residual_rows.reshape(-1)
    return (current, projected_rows, residual_rows)


def solution(mesh):
    in_specs = (P("band", "grid", None, None), P("grid", None, None))
    out_specs = (P("band", "grid", None, None), P("band", None), P("band"))
    return jax.shard_map(
        on_device, mesh=mesh, in_specs=in_specs, out_specs=out_specs, check_vma=False
    )
```

```python
import jax
import jax.numpy as jnp
from jax import lax
from jax.experimental import pallas as pl
from jax.experimental.pallas import tpu as pltpu
from jax.sharding import PartitionSpec as P

CENTER = 4.25
HALF_WIDTH = 3.75
LOWEST = -2.0
SIGMA_ONE = HALF_WIDTH / (LOWEST - CENTER)
FOUR_THIRDS = 4.0 / 3.0
TWELFTH = 1.0 / 12.0
filter_degree = 4


def butterfly_sum(values, axis, partner_rounds):
    count = lax.axis_size(axis)
    for partner in partner_rounds:
        pairs = [(i, partner(i)) for i in range(count)]
        values = values + lax.ppermute(values, axis, pairs)
    return values


def flip(bit):
    return lambda i: i ^ bit


def ring_of_four(low, stride):
    def partner(i):
        place = (i // stride) % 4
        return i + (3 - 2 * place) * stride

    return partner


def filter_kernel(below_ref, own_ref, above_ref, below_pot, own_pot, above_pot, filtered_ref, image_ref,
                  first_buf, second_buf, third_buf, wide_pot):
    band_count, own_planes = filtered_ref.shape[0], filtered_ref.shape[1]
    width = below_ref.shape[1]
    for at, source, pot in ((0, below_ref, below_pot), (width, own_ref, own_pot),
                            (width + own_planes, above_ref, above_pot)):
        first_buf[:, at : at + source.shape[1]] = source[...]
        wide_pot[at : at + source.shape[1]] = pot[...]
    rows, lanes = first_buf.shape[2], first_buf.shape[3]

    def apply(field, band, plane):
        centre = field[band, plane]
        near_sum = field[band, plane - 1] + field[band, plane + 1]
        near_sum = near_sum + pltpu.roll(centre, 1, 0) + pltpu.roll(centre, rows - 1, 0)
        near_sum = near_sum + pltpu.roll(centre, 1, 1) + pltpu.roll(centre, lanes - 1, 1)
        far_sum = field[band, plane - 2] + field[band, plane + 2]
        far_sum = far_sum + pltpu.roll(centre, 2, 0) + pltpu.roll(centre, rows - 2, 0)
        far_sum = far_sum + pltpu.roll(centre, 2, 1) + pltpu.roll(centre, lanes - 2, 1)
        kinetic = 0.5 * (7.5 * centre - FOUR_THIRDS * near_sum + TWELFTH * far_sum)
        return kinetic + wide_pot[plane] * centre, centre

    def sweep(field, older, out, lo, hi, scale, carry_scale):
        for plane in range(lo, hi):
            for band in range(band_count):
                applied, centre = apply(field, band, plane)
                value = (applied - CENTER * centre) * scale
                if older is not None:
                    value = value - carry_scale * older[band, plane]
                out[band, plane] = value

    total = first_buf.shape[1]
    sweep(first_buf, None, second_buf, 2, total - 2, SIGMA_ONE / HALF_WIDTH, 0.0)
    bufs = [first_buf, second_buf, third_buf]
    older, field, spare = 0, 1, 2
    sigma_now = SIGMA_ONE
    for repeat_index in range(filter_degree - 1):
        sigma_next = 1.0 / (2.0 / SIGMA_ONE - sigma_now)
        margin = 2 * (repeat_index + 2)
        sweep(bufs[field], bufs[older], bufs[spare], margin, total - margin,
              2.0 * sigma_next / HALF_WIDTH, sigma_now * sigma_next)
        older, field, spare = field, spare, older
        sigma_now = sigma_next
    final = bufs[field]
    filtered_ref[...] = final[:, width : width + own_planes]

    for plane in range(width, width + own_planes):
        for band in range(band_count):
            image_ref[band, plane - width], _ = apply(final, band, plane)


def filter_and_image(below, own, above, below_pot, own_pot, above_pot):
    band_count = own.shape[0]
    own_planes, rows, lanes = own.shape[1], own.shape[2], own.shape[3]
    total = below.shape[1] + own_planes + above.shape[1]
    shape = (band_count, own_planes, rows, lanes)
    cells = band_count * total * rows * lanes
    return pl.pallas_call(
        filter_kernel,
        out_shape=(jax.ShapeDtypeStruct(shape, jnp.float32), jax.ShapeDtypeStruct(shape, jnp.float32)),
        in_specs=[pl.BlockSpec(memory_space=pltpu.VMEM)] * 6,
        out_specs=(pl.BlockSpec(memory_space=pltpu.VMEM), pl.BlockSpec(memory_space=pltpu.VMEM)),
        scratch_shapes=[pltpu.VMEM((band_count, total, rows, lanes), jnp.float32)] * 3
        + [pltpu.VMEM((total, rows, lanes), jnp.float32)],
        cost_estimate=pl.CostEstimate(flops=30 * cells * 4, transcendentals=0, bytes_accessed=4 * cells * 3),
    )(below, own, above, below_pot, own_pot, above_pot)


def rayleigh_ritz_kernel(first_ref, margin_ref, subspace_ref, norms_ref, projected_ref, residual_ref,
                         projected_buf, residual_buf):
    size = margin_ref.shape[0]
    work = margin_ref[...]
    rest = subspace_ref[...]
    rows = lax.broadcasted_iota(jnp.int32, (size, size), 0)
    cols = lax.broadcasted_iota(jnp.int32, (size, size), 1)
    row_index = rows[:, :1]
    col_index = cols[:1, :]
    coeff_t = jnp.zeros((size, size), jnp.float32)
    columns, inverses = [], []
    for k in range(size):
        inverse = 1.0 / jnp.sqrt(work[k : k + 1, k : k + 1])
        column = jnp.where(row_index >= k, work[:, k : k + 1] * inverse, 0.0)
        row = jnp.where(col_index >= k, work[k : k + 1, :] * inverse, 0.0)
        work = work - column * row
        solved = rest[:, k : k + 1] * inverse
        rest = rest - solved * jnp.where(col_index > k, row, 0.0)
        coeff_t = jnp.where(cols == k, solved, coeff_t)
        columns.append(jnp.where(row_index > k, column, 0.0))
        inverses.append(inverse)
    rest = coeff_t
    projected = jnp.zeros((size, size), jnp.float32)
    for i in range(size):
        row = rest[i : i + 1, :] * inverses[i]
        rest = rest - columns[i] * row
        projected = jnp.where(rows == i, row, projected)
    projected_buf[...] = projected
    residual_buf[...] = norms_ref[...] - jnp.sum(coeff_t * coeff_t, axis=1, keepdims=True)
    first = first_ref[0]
    count = projected_ref.shape[0]
    projected_ref[...] = projected_buf[pl.ds(first, count), :]
    residual_ref[...] = residual_buf[pl.ds(first, count), :]


def rayleigh_ritz(first_band, band_count, margin, subspace, image_norms):
    size = margin.shape[0]
    return pl.pallas_call(
        rayleigh_ritz_kernel,
        out_shape=(jax.ShapeDtypeStruct((band_count, size), jnp.float32),
                   jax.ShapeDtypeStruct((band_count, 1), jnp.float32)),
        in_specs=[pl.BlockSpec(memory_space=pltpu.SMEM)] + [pl.BlockSpec(memory_space=pltpu.VMEM)] * 3,
        out_specs=(pl.BlockSpec(memory_space=pltpu.VMEM), pl.BlockSpec(memory_space=pltpu.VMEM)),
        scratch_shapes=[pltpu.VMEM((size, size), jnp.float32), pltpu.VMEM((size, 1), jnp.float32)],
        cost_estimate=pl.CostEstimate(flops=6 * size**3, transcendentals=size, bytes_accessed=4 * 4 * size * size),
    )(first_band.reshape(1).astype(jnp.int32), margin, subspace, image_norms.reshape(size, 1))


def replica_pairs(direction):
    grid_count, band_count = lax.axis_size("grid"), lax.axis_size("band")
    pairs = []
    for target_grid in range(grid_count):
        source_grid = (target_grid - direction) % grid_count
        far = source_grid // 8 != target_grid // 8
        for target_band in range(band_count):
            source_band = target_band ^ 4 if far else target_band
            pairs.append((source_band * grid_count + source_grid, target_band * grid_count + target_grid))
    return pairs


def on_device(trial_bands, potential):
    band_count = trial_bands.shape[0]
    width = 2 * (filter_degree + 1)
    count = lax.axis_size("grid")
    below = lax.ppermute(trial_bands[:, trial_bands.shape[1] - width :], "grid", [(i, (i + 1) % count) for i in range(count)])
    above = lax.ppermute(trial_bands[:, :width], "grid", [((i + 1) % count, i) for i in range(count)])
    below_pot = lax.ppermute(potential[potential.shape[0] - width :], ("band", "grid"), replica_pairs(1))
    above_pot = lax.ppermute(potential[:width], ("band", "grid"), replica_pairs(-1))
    current, applied = filter_and_image(below, trial_bands, above, below_pot, potential, above_pot)
    band_devices = lax.axis_size("band")
    total_bands = band_count * band_devices
    cell_count = current.shape[1] * current.shape[2] * current.shape[3]
    cell_total = cell_count * lax.axis_size("grid")
    inverse_cells = 1.0 / cell_total
    first_band = lax.axis_index("band") * band_count
    both = jnp.stack(
        [current.reshape(band_count, cell_count), applied.reshape(band_count, cell_count)]
    ).reshape(2, band_count, band_devices, cell_count // band_devices)
    moved = lax.all_to_all(both, "band", 2, 1, tiled=True)
    bands_here = moved[0].reshape(total_bands, -1)
    image_here = moved[1].reshape(total_bands, -1)
    margin_part = jnp.dot(
        bands_here, bands_here.T, precision=lax.Precision.HIGHEST, preferred_element_type=jnp.float32
    )
    image_part = jnp.dot(
        image_here, bands_here.T, precision=lax.Precision.HIGHEST, preferred_element_type=jnp.float32
    )
    norm_part = jnp.sum(image_here * image_here, axis=1)
    packed = jnp.concatenate([margin_part.reshape(-1), image_part.reshape(-1), norm_part])
    packed = butterfly_sum(packed, "band", [flip(8), ring_of_four(0, 8), flip(1), flip(2), flip(4)])
    packed = butterfly_sum(packed, "grid", [flip(1), flip(2), ring_of_four(0, 2), flip(8)])
    packed = packed * inverse_cells
    square = total_bands * total_bands
    margin = packed[:square].reshape(total_bands, total_bands)
    subspace = packed[square : 2 * square].reshape(total_bands, total_bands)
    image_norms = packed[2 * square :]
    margin = (margin + margin.T) / 2
    projected_rows, residual_rows = rayleigh_ritz(first_band, band_count, margin, subspace, image_norms)
    residual_rows = residual_rows.reshape(-1)
    return (current, projected_rows, residual_rows)


def solution(mesh):
    in_specs = (P("band", "grid", None, None), P("grid", None, None))
    out_specs = (P("band", "grid", None, None), P("band", None), P("band"))
    return jax.shard_map(
        on_device, mesh=mesh, in_specs=in_specs, out_specs=out_specs, check_vma=False
    )
```

```python
import jax
import jax.numpy as jnp
from jax import lax
from jax.experimental import pallas as pl
from jax.experimental.pallas import tpu as pltpu
from jax.sharding import PartitionSpec as P

CENTER = 4.25
HALF_WIDTH = 3.75
LOWEST = -2.0
SIGMA_ONE = HALF_WIDTH / (LOWEST - CENTER)
FOUR_THIRDS = 4.0 / 3.0
TWELFTH = 1.0 / 12.0
filter_degree = 4


def butterfly_sum(values, axis, partner_rounds):
    count = lax.axis_size(axis)
    for partner in partner_rounds:
        pairs = [(i, partner(i)) for i in range(count)]
        values = values + lax.ppermute(values, axis, pairs)
    return values


def flip(bit):
    return lambda i: i ^ bit


def ring_of_four(low, stride):
    def partner(i):
        place = (i // stride) % 4
        return i + (3 - 2 * place) * stride

    return partner


def filter_kernel(below_ref, own_ref, above_ref, below_pot, own_pot, above_pot, filtered_ref, image_ref,
                  first_buf, second_buf, third_buf, wide_pot):
    band_count, own_planes = filtered_ref.shape[0], filtered_ref.shape[1]
    width = below_ref.shape[1]
    for at, source, pot in ((0, below_ref, below_pot), (width, own_ref, own_pot),
                            (width + own_planes, above_ref, above_pot)):
        pltpu.sync_copy(source, first_buf.at[:, at : at + source.shape[1]])
        pltpu.sync_copy(pot, wide_pot.at[at : at + pot.shape[0]])
    rows, lanes = first_buf.shape[2], first_buf.shape[3]

    def apply(field, band, plane):
        centre = field[band, plane]
        near_sum = field[band, plane - 1] + field[band, plane + 1]
        near_sum = near_sum + pltpu.roll(centre, 1, 0) + pltpu.roll(centre, rows - 1, 0)
        near_sum = near_sum + pltpu.roll(centre, 1, 1) + pltpu.roll(centre, lanes - 1, 1)
        far_sum = field[band, plane - 2] + field[band, plane + 2]
        far_sum = far_sum + pltpu.roll(centre, 2, 0) + pltpu.roll(centre, rows - 2, 0)
        far_sum = far_sum + pltpu.roll(centre, 2, 1) + pltpu.roll(centre, lanes - 2, 1)
        kinetic = 0.5 * (7.5 * centre - FOUR_THIRDS * near_sum + TWELFTH * far_sum)
        return kinetic + wide_pot[plane] * centre, centre

    def sweep(field, older, out, lo, hi, scale, carry_scale):
        for plane in range(lo, hi):
            for band in range(band_count):
                applied, centre = apply(field, band, plane)
                value = (applied - CENTER * centre) * scale
                if older is not None:
                    value = value - carry_scale * older[band, plane]
                out[band, plane] = value

    total = first_buf.shape[1]
    sweep(first_buf, None, second_buf, 2, total - 2, SIGMA_ONE / HALF_WIDTH, 0.0)
    bufs = [first_buf, second_buf, third_buf]
    older, field, spare = 0, 1, 2
    sigma_now = SIGMA_ONE
    for repeat_index in range(filter_degree - 1):
        sigma_next = 1.0 / (2.0 / SIGMA_ONE - sigma_now)
        margin = 2 * (repeat_index + 2)
        sweep(bufs[field], bufs[older], bufs[spare], margin, total - margin,
              2.0 * sigma_next / HALF_WIDTH, sigma_now * sigma_next)
        older, field, spare = field, spare, older
        sigma_now = sigma_next
    final = bufs[field]
    filtered_ref[...] = final[:, width : width + own_planes]

    for plane in range(width, width + own_planes):
        for band in range(band_count):
            image_ref[band, plane - width], _ = apply(final, band, plane)


def filter_and_image(below, own, above, below_pot, own_pot, above_pot):
    band_count = own.shape[0]
    own_planes, rows, lanes = own.shape[1], own.shape[2], own.shape[3]
    total = below.shape[1] + own_planes + above.shape[1]
    shape = (band_count, own_planes, rows, lanes)
    cells = band_count * total * rows * lanes
    return pl.pallas_call(
        filter_kernel,
        out_shape=(jax.ShapeDtypeStruct(shape, jnp.float32), jax.ShapeDtypeStruct(shape, jnp.float32)),
        in_specs=[pl.BlockSpec(memory_space=pl.ANY)] * 6,
        out_specs=(pl.BlockSpec(memory_space=pltpu.VMEM), pl.BlockSpec(memory_space=pltpu.VMEM)),
        scratch_shapes=[pltpu.VMEM((band_count, total, rows, lanes), jnp.float32)] * 3
        + [pltpu.VMEM((total, rows, lanes), jnp.float32)],
        cost_estimate=pl.CostEstimate(flops=30 * cells * 4, transcendentals=0, bytes_accessed=4 * cells * 3),
    )(below, own, above, below_pot, own_pot, above_pot)


def rayleigh_ritz_kernel(first_ref, margin_ref, subspace_ref, norms_ref, projected_ref, residual_ref,
                         projected_buf, residual_buf):
    size = margin_ref.shape[0]
    work = margin_ref[...]
    rest = subspace_ref[...]
    rows = lax.broadcasted_iota(jnp.int32, (size, size), 0)
    cols = lax.broadcasted_iota(jnp.int32, (size, size), 1)
    row_index = rows[:, :1]
    col_index = cols[:1, :]
    coeff_t = jnp.zeros((size, size), jnp.float32)
    columns, inverses = [], []
    for k in range(size):
        inverse = 1.0 / jnp.sqrt(work[k : k + 1, k : k + 1])
        column = jnp.where(row_index >= k, work[:, k : k + 1] * inverse, 0.0)
        row = jnp.where(col_index >= k, work[k : k + 1, :] * inverse, 0.0)
        work = work - column * row
        solved = rest[:, k : k + 1] * inverse
        rest = rest - solved * jnp.where(col_index > k, row, 0.0)
        coeff_t = jnp.where(cols == k, solved, coeff_t)
        columns.append(jnp.where(row_index > k, column, 0.0))
        inverses.append(inverse)
    rest = coeff_t
    projected = jnp.zeros((size, size), jnp.float32)
    for i in range(size):
        row = rest[i : i + 1, :] * inverses[i]
        rest = rest - columns[i] * row
        projected = jnp.where(rows == i, row, projected)
    projected_buf[...] = projected
    residual_buf[...] = norms_ref[...] - jnp.sum(coeff_t * coeff_t, axis=1, keepdims=True)
    first = first_ref[0]
    count = projected_ref.shape[0]
    projected_ref[...] = projected_buf[pl.ds(first, count), :]
    residual_ref[...] = residual_buf[pl.ds(first, count), :]


def rayleigh_ritz(first_band, band_count, margin, subspace, image_norms):
    size = margin.shape[0]
    return pl.pallas_call(
        rayleigh_ritz_kernel,
        out_shape=(jax.ShapeDtypeStruct((band_count, size), jnp.float32),
                   jax.ShapeDtypeStruct((band_count, 1), jnp.float32)),
        in_specs=[pl.BlockSpec(memory_space=pltpu.SMEM)] + [pl.BlockSpec(memory_space=pltpu.VMEM)] * 3,
        out_specs=(pl.BlockSpec(memory_space=pltpu.VMEM), pl.BlockSpec(memory_space=pltpu.VMEM)),
        scratch_shapes=[pltpu.VMEM((size, size), jnp.float32), pltpu.VMEM((size, 1), jnp.float32)],
        cost_estimate=pl.CostEstimate(flops=6 * size**3, transcendentals=size, bytes_accessed=4 * 4 * size * size),
    )(first_band.reshape(1).astype(jnp.int32), margin, subspace, image_norms.reshape(size, 1))


def replica_pairs(direction):
    grid_count, band_count = lax.axis_size("grid"), lax.axis_size("band")
    pairs = []
    for target_grid in range(grid_count):
        source_grid = (target_grid - direction) % grid_count
        far = source_grid // 8 != target_grid // 8
        for target_band in range(band_count):
            source_band = target_band ^ 4 if far else target_band
            pairs.append((source_band * grid_count + source_grid, target_band * grid_count + target_grid))
    return pairs


def on_device(trial_bands, potential):
    band_count = trial_bands.shape[0]
    width = 2 * (filter_degree + 1)
    count = lax.axis_size("grid")
    below = lax.ppermute(trial_bands[:, trial_bands.shape[1] - width :], "grid", [(i, (i + 1) % count) for i in range(count)])
    above = lax.ppermute(trial_bands[:, :width], "grid", [((i + 1) % count, i) for i in range(count)])
    below_pot = lax.ppermute(potential[potential.shape[0] - width :], ("band", "grid"), replica_pairs(1))
    above_pot = lax.ppermute(potential[:width], ("band", "grid"), replica_pairs(-1))
    current, applied = filter_and_image(below, trial_bands, above, below_pot, potential, above_pot)
    band_devices = lax.axis_size("band")
    total_bands = band_count * band_devices
    cell_count = current.shape[1] * current.shape[2] * current.shape[3]
    cell_total = cell_count * lax.axis_size("grid")
    inverse_cells = 1.0 / cell_total
    first_band = lax.axis_index("band") * band_count
    both = jnp.stack(
        [current.reshape(band_count, cell_count), applied.reshape(band_count, cell_count)]
    ).reshape(2, band_count, band_devices, cell_count // band_devices)
    moved = lax.all_to_all(both, "band", 2, 1, tiled=True)
    bands_here = moved[0].reshape(total_bands, -1)
    image_here = moved[1].reshape(total_bands, -1)
    margin_part = jnp.dot(
        bands_here, bands_here.T, precision=lax.Precision.HIGHEST, preferred_element_type=jnp.float32
    )
    image_part = jnp.dot(
        image_here, bands_here.T, precision=lax.Precision.HIGHEST, preferred_element_type=jnp.float32
    )
    norm_part = jnp.sum(image_here * image_here, axis=1)
    packed = jnp.concatenate([margin_part.reshape(-1), image_part.reshape(-1), norm_part])
    packed = butterfly_sum(packed, "band", [flip(1), flip(2), flip(4), flip(8), ring_of_four(0, 8)])
    packed = butterfly_sum(packed, "grid", [flip(1), flip(2), ring_of_four(0, 2), flip(8)])
    packed = packed * inverse_cells
    square = total_bands * total_bands
    margin = packed[:square].reshape(total_bands, total_bands)
    subspace = packed[square : 2 * square].reshape(total_bands, total_bands)
    image_norms = packed[2 * square :]
    margin = (margin + margin.T) / 2
    projected_rows, residual_rows = rayleigh_ritz(first_band, band_count, margin, subspace, image_norms)
    residual_rows = residual_rows.reshape(-1)
    return (current, projected_rows, residual_rows)


def solution(mesh):
    in_specs = (P("band", "grid", None, None), P("grid", None, None))
    out_specs = (P("band", "grid", None, None), P("band", None), P("band"))
    return jax.shard_map(
        on_device, mesh=mesh, in_specs=in_specs, out_specs=out_specs, check_vma=False
    )
```

```python
import jax
import jax.numpy as jnp
from jax import lax
from jax.experimental import pallas as pl
from jax.experimental.pallas import tpu as pltpu
from jax.sharding import PartitionSpec as P

CENTER = 4.25
HALF_WIDTH = 3.75
LOWEST = -2.0
SIGMA_ONE = HALF_WIDTH / (LOWEST - CENTER)
FOUR_THIRDS = 4.0 / 3.0
TWELFTH = 1.0 / 12.0
filter_degree = 4


def butterfly_sum(values, axis, partner_rounds):
    count = lax.axis_size(axis)
    for partner in partner_rounds:
        pairs = [(i, partner(i)) for i in range(count)]
        values = values + lax.ppermute(values, axis, pairs)
    return values


def flip(bit):
    return lambda i: i ^ bit


def ring_of_four(low, stride):
    def partner(i):
        place = (i // stride) % 4
        return i + (3 - 2 * place) * stride

    return partner


def filter_kernel(below_ref, own_ref, above_ref, below_pot, own_pot, above_pot, filtered_ref, image_ref,
                  first_buf, second_buf, third_buf, wide_pot):
    band_count, own_planes = filtered_ref.shape[0], filtered_ref.shape[1]
    width = below_ref.shape[1]
    for at, source, pot in ((0, below_ref, below_pot), (width, own_ref, own_pot),
                            (width + own_planes, above_ref, above_pot)):
        first_buf[:, at : at + source.shape[1]] = source[...]
        wide_pot[at : at + source.shape[1]] = pot[...]
    rows, lanes = first_buf.shape[2], first_buf.shape[3]

    def apply(field, band, plane):
        centre = field[band, plane]
        near_sum = field[band, plane - 1] + field[band, plane + 1]
        near_sum = near_sum + pltpu.roll(centre, 1, 0) + pltpu.roll(centre, rows - 1, 0)
        near_sum = near_sum + pltpu.roll(centre, 1, 1) + pltpu.roll(centre, lanes - 1, 1)
        far_sum = field[band, plane - 2] + field[band, plane + 2]
        far_sum = far_sum + pltpu.roll(centre, 2, 0) + pltpu.roll(centre, rows - 2, 0)
        far_sum = far_sum + pltpu.roll(centre, 2, 1) + pltpu.roll(centre, lanes - 2, 1)
        kinetic = 0.5 * (7.5 * centre - FOUR_THIRDS * near_sum + TWELFTH * far_sum)
        return kinetic + wide_pot[plane] * centre, centre

    def sweep(field, older, out, lo, hi, scale, carry_scale):
        for plane in range(lo, hi):
            for band in range(band_count):
                applied, centre = apply(field, band, plane)
                value = (applied - CENTER * centre) * scale
                if older is not None:
                    value = value - carry_scale * older[band, plane]
                out[band, plane] = value

    total = first_buf.shape[1]
    sweep(first_buf, None, second_buf, 2, total - 2, SIGMA_ONE / HALF_WIDTH, 0.0)
    bufs = [first_buf, second_buf, third_buf]
    older, field, spare = 0, 1, 2
    sigma_now = SIGMA_ONE
    for repeat_index in range(filter_degree - 1):
        sigma_next = 1.0 / (2.0 / SIGMA_ONE - sigma_now)
        margin = 2 * (repeat_index + 2)
        sweep(bufs[field], bufs[older], bufs[spare], margin, total - margin,
              2.0 * sigma_next / HALF_WIDTH, sigma_now * sigma_next)
        older, field, spare = field, spare, older
        sigma_now = sigma_next
    final = bufs[field]
    filtered_ref[...] = final[:, width : width + own_planes]

    for plane in range(width, width + own_planes):
        for band in range(band_count):
            image_ref[band, plane - width], _ = apply(final, band, plane)


def filter_and_image(below, own, above, below_pot, own_pot, above_pot):
    band_count = own.shape[0]
    own_planes, rows, lanes = own.shape[1], own.shape[2], own.shape[3]
    total = below.shape[1] + own_planes + above.shape[1]
    shape = (band_count, own_planes, rows, lanes)
    cells = band_count * total * rows * lanes
    return pl.pallas_call(
        filter_kernel,
        out_shape=(jax.ShapeDtypeStruct(shape, jnp.float32), jax.ShapeDtypeStruct(shape, jnp.float32)),
        in_specs=[pl.BlockSpec(memory_space=pltpu.VMEM)] * 6,
        out_specs=(pl.BlockSpec(memory_space=pltpu.VMEM), pl.BlockSpec(memory_space=pltpu.VMEM)),
        scratch_shapes=[pltpu.VMEM((band_count, total, rows, lanes), jnp.float32)] * 3
        + [pltpu.VMEM((total, rows, lanes), jnp.float32)],
        cost_estimate=pl.CostEstimate(flops=30 * cells * 4, transcendentals=0, bytes_accessed=4 * cells * 3),
    )(below, own, above, below_pot, own_pot, above_pot)


def rayleigh_ritz_kernel(first_ref, margin_ref, subspace_ref, norms_ref, projected_ref, residual_ref,
                         projected_buf, residual_buf):
    size = margin_ref.shape[0]
    work = margin_ref[...]
    rest = subspace_ref[...]
    rows = lax.broadcasted_iota(jnp.int32, (size, size), 0)
    cols = lax.broadcasted_iota(jnp.int32, (size, size), 1)
    row_index = rows[:, :1]
    col_index = cols[:1, :]
    coeff_t = jnp.zeros((size, size), jnp.float32)
    columns, inverses = [], []
    for k in range(size):
        inverse = 1.0 / jnp.sqrt(work[k : k + 1, k : k + 1])
        column = jnp.where(row_index >= k, work[:, k : k + 1] * inverse, 0.0)
        row = jnp.where(col_index >= k, work[k : k + 1, :] * inverse, 0.0)
        work = work - column * row
        solved = rest[:, k : k + 1] * inverse
        rest = rest - solved * jnp.where(col_index > k, row, 0.0)
        coeff_t = jnp.where(cols == k, solved, coeff_t)
        columns.append(jnp.where(row_index > k, column, 0.0))
        inverses.append(inverse)
    rest = coeff_t
    projected = jnp.zeros((size, size), jnp.float32)
    for i in range(size):
        row = rest[i : i + 1, :] * inverses[i]
        rest = rest - columns[i] * row
        projected = jnp.where(rows == i, row, projected)
    projected_buf[...] = projected
    residual_buf[...] = norms_ref[...] - jnp.sum(coeff_t * coeff_t, axis=1, keepdims=True)
    first = first_ref[0]
    count = projected_ref.shape[0]
    projected_ref[...] = projected_buf[pl.ds(first, count), :]
    picked = jnp.broadcast_to(residual_buf[pl.ds(first, count), :], (count, count))
    diagonal = lax.broadcasted_iota(jnp.int32, (count, count), 0) == lax.broadcasted_iota(jnp.int32, (count, count), 1)
    residual_ref[...] = jnp.sum(jnp.where(diagonal, picked, 0.0), axis=0, keepdims=True)


def rayleigh_ritz(first_band, band_count, margin, subspace, image_norms):
    size = margin.shape[0]
    return pl.pallas_call(
        rayleigh_ritz_kernel,
        out_shape=(jax.ShapeDtypeStruct((band_count, size), jnp.float32),
                   jax.ShapeDtypeStruct((1, band_count), jnp.float32)),
        in_specs=[pl.BlockSpec(memory_space=pltpu.SMEM)] + [pl.BlockSpec(memory_space=pltpu.VMEM)] * 3,
        out_specs=(pl.BlockSpec(memory_space=pltpu.VMEM), pl.BlockSpec(memory_space=pltpu.VMEM)),
        scratch_shapes=[pltpu.VMEM((size, size), jnp.float32), pltpu.VMEM((size, 1), jnp.float32)],
        cost_estimate=pl.CostEstimate(flops=6 * size**3, transcendentals=size, bytes_accessed=4 * 4 * size * size),
    )(first_band.reshape(1).astype(jnp.int32), margin, subspace, image_norms.reshape(size, 1))


def replica_pairs(direction):
    grid_count, band_count = lax.axis_size("grid"), lax.axis_size("band")
    pairs = []
    for target_grid in range(grid_count):
        source_grid = (target_grid - direction) % grid_count
        far = source_grid // 8 != target_grid // 8
        for target_band in range(band_count):
            source_band = target_band ^ 4 if far else target_band
            pairs.append((source_band * grid_count + source_grid, target_band * grid_count + target_grid))
    return pairs


def on_device(trial_bands, potential):
    band_count = trial_bands.shape[0]
    width = 2 * (filter_degree + 1)
    count = lax.axis_size("grid")
    below = lax.ppermute(trial_bands[:, trial_bands.shape[1] - width :], "grid", [(i, (i + 1) % count) for i in range(count)])
    above = lax.ppermute(trial_bands[:, :width], "grid", [((i + 1) % count, i) for i in range(count)])
    below_pot = lax.ppermute(potential[potential.shape[0] - width :], ("band", "grid"), replica_pairs(1))
    above_pot = lax.ppermute(potential[:width], ("band", "grid"), replica_pairs(-1))
    current, applied = filter_and_image(below, trial_bands, above, below_pot, potential, above_pot)
    band_devices = lax.axis_size("band")
    total_bands = band_count * band_devices
    cell_count = current.shape[1] * current.shape[2] * current.shape[3]
    cell_total = cell_count * lax.axis_size("grid")
    inverse_cells = 1.0 / cell_total
    first_band = lax.axis_index("band") * band_count
    both = jnp.stack(
        [current.reshape(band_count, cell_count), applied.reshape(band_count, cell_count)]
    ).reshape(2, band_count, band_devices, cell_count // band_devices)
    moved = lax.all_to_all(both, "band", 2, 1, tiled=True)
    bands_here = moved[0].reshape(total_bands, -1)
    image_here = moved[1].reshape(total_bands, -1)
    margin_part = jnp.dot(
        bands_here, bands_here.T, precision=lax.Precision.HIGHEST, preferred_element_type=jnp.float32
    )
    image_part = jnp.dot(
        image_here, bands_here.T, precision=lax.Precision.HIGHEST, preferred_element_type=jnp.float32
    )
    norm_part = jnp.sum(image_here * image_here, axis=1)
    packed = jnp.concatenate([margin_part.reshape(-1), image_part.reshape(-1), norm_part])
    packed = butterfly_sum(packed, "band", [flip(1), flip(2), flip(4), flip(8), ring_of_four(0, 8)])
    packed = butterfly_sum(packed, "grid", [flip(1), flip(2), ring_of_four(0, 2), flip(8)])
    packed = packed * inverse_cells
    square = total_bands * total_bands
    margin = packed[:square].reshape(total_bands, total_bands)
    subspace = packed[square : 2 * square].reshape(total_bands, total_bands)
    image_norms = packed[2 * square :]
    margin = (margin + margin.T) / 2
    projected_rows, residual_rows = rayleigh_ritz(first_band, band_count, margin, subspace, image_norms)
    residual_rows = residual_rows.reshape(-1)
    return (current, projected_rows, residual_rows)


def solution(mesh):
    in_specs = (P("band", "grid", None, None), P("grid", None, None))
    out_specs = (P("band", "grid", None, None), P("band", None), P("band"))
    return jax.shard_map(
        on_device, mesh=mesh, in_specs=in_specs, out_specs=out_specs, check_vma=False
    )
```

```python
import jax
import jax.numpy as jnp
from jax import lax
from jax.experimental import pallas as pl
from jax.experimental.pallas import tpu as pltpu
from jax.sharding import PartitionSpec as P

CENTER = 4.25
HALF_WIDTH = 3.75
LOWEST = -2.0
SIGMA_ONE = HALF_WIDTH / (LOWEST - CENTER)
FOUR_THIRDS = 4.0 / 3.0
TWELFTH = 1.0 / 12.0
filter_degree = 4


def butterfly_sum(values, axis, partner_rounds):
    count = lax.axis_size(axis)
    for partner in partner_rounds:
        pairs = [(i, partner(i)) for i in range(count)]
        values = values + lax.ppermute(values, axis, pairs)
    return values


def flip(bit):
    return lambda i: i ^ bit


def ring_of_four(low, stride):
    def partner(i):
        place = (i // stride) % 4
        return i + (3 - 2 * place) * stride

    return partner


def filter_kernel(below_ref, own_ref, above_ref, below_pot, own_pot, above_pot, both_ref,
                  first_buf, second_buf, third_buf, wide_pot):
    band_count, own_planes = both_ref.shape[1], both_ref.shape[2]
    width = below_ref.shape[1]
    for at, source, pot in ((0, below_ref, below_pot), (width, own_ref, own_pot),
                            (width + own_planes, above_ref, above_pot)):
        first_buf[:, at : at + source.shape[1]] = source[...]
        wide_pot[at : at + source.shape[1]] = pot[...]
    rows, lanes = first_buf.shape[2], first_buf.shape[3]

    def apply(field, band, plane):
        centre = field[band, plane]
        near_sum = field[band, plane - 1] + field[band, plane + 1]
        near_sum = near_sum + pltpu.roll(centre, 1, 0) + pltpu.roll(centre, rows - 1, 0)
        near_sum = near_sum + pltpu.roll(centre, 1, 1) + pltpu.roll(centre, lanes - 1, 1)
        far_sum = field[band, plane - 2] + field[band, plane + 2]
        far_sum = far_sum + pltpu.roll(centre, 2, 0) + pltpu.roll(centre, rows - 2, 0)
        far_sum = far_sum + pltpu.roll(centre, 2, 1) + pltpu.roll(centre, lanes - 2, 1)
        kinetic = 0.5 * (7.5 * centre - FOUR_THIRDS * near_sum + TWELFTH * far_sum)
        return kinetic + wide_pot[plane] * centre, centre

    def sweep(field, older, out, lo, hi, scale, carry_scale):
        for plane in range(lo, hi):
            for band in range(band_count):
                applied, centre = apply(field, band, plane)
                value = (applied - CENTER * centre) * scale
                if older is not None:
                    value = value - carry_scale * older[band, plane]
                out[band, plane] = value

    total = first_buf.shape[1]
    sweep(first_buf, None, second_buf, 2, total - 2, SIGMA_ONE / HALF_WIDTH, 0.0)
    bufs = [first_buf, second_buf, third_buf]
    older, field, spare = 0, 1, 2
    sigma_now = SIGMA_ONE
    for repeat_index in range(filter_degree - 1):
        sigma_next = 1.0 / (2.0 / SIGMA_ONE - sigma_now)
        margin = 2 * (repeat_index + 2)
        sweep(bufs[field], bufs[older], bufs[spare], margin, total - margin,
              2.0 * sigma_next / HALF_WIDTH, sigma_now * sigma_next)
        older, field, spare = field, spare, older
        sigma_now = sigma_next
    final = bufs[field]
    both_ref[0] = final[:, width : width + own_planes]

    for plane in range(width, width + own_planes):
        for band in range(band_count):
            both_ref[1, band, plane - width], _ = apply(final, band, plane)


def filter_and_image(below, own, above, below_pot, own_pot, above_pot):
    band_count = own.shape[0]
    own_planes, rows, lanes = own.shape[1], own.shape[2], own.shape[3]
    total = below.shape[1] + own_planes + above.shape[1]
    shape = (band_count, own_planes, rows, lanes)
    cells = band_count * total * rows * lanes
    return pl.pallas_call(
        filter_kernel,
        out_shape=jax.ShapeDtypeStruct((2, *shape), jnp.float32),
        in_specs=[pl.BlockSpec(memory_space=pltpu.VMEM)] * 6,
        out_specs=pl.BlockSpec(memory_space=pltpu.VMEM),
        scratch_shapes=[pltpu.VMEM((band_count, total, rows, lanes), jnp.float32)] * 3
        + [pltpu.VMEM((total, rows, lanes), jnp.float32)],
        cost_estimate=pl.CostEstimate(flops=30 * cells * 4, transcendentals=0, bytes_accessed=4 * cells * 3),
    )(below, own, above, below_pot, own_pot, above_pot)


def rayleigh_ritz_kernel(first_ref, margin_ref, subspace_ref, norms_ref, projected_ref, residual_ref,
                         projected_buf, residual_buf):
    size = margin_ref.shape[0]
    work = margin_ref[...]
    rest = subspace_ref[...]
    rows = lax.broadcasted_iota(jnp.int32, (size, size), 0)
    cols = lax.broadcasted_iota(jnp.int32, (size, size), 1)
    row_index = rows[:, :1]
    col_index = cols[:1, :]
    coeff_t = jnp.zeros((size, size), jnp.float32)
    columns, inverses = [], []
    for k in range(size):
        inverse = 1.0 / jnp.sqrt(work[k : k + 1, k : k + 1])
        column = jnp.where(row_index >= k, work[:, k : k + 1] * inverse, 0.0)
        row = jnp.where(col_index >= k, work[k : k + 1, :] * inverse, 0.0)
        work = work - column * row
        solved = rest[:, k : k + 1] * inverse
        rest = rest - solved * jnp.where(col_index > k, row, 0.0)
        coeff_t = jnp.where(cols == k, solved, coeff_t)
        columns.append(jnp.where(row_index > k, column, 0.0))
        inverses.append(inverse)
    rest = coeff_t
    projected = jnp.zeros((size, size), jnp.float32)
    for i in range(size):
        row = rest[i : i + 1, :] * inverses[i]
        rest = rest - columns[i] * row
        projected = jnp.where(rows == i, row, projected)
    projected_buf[...] = projected
    residual_buf[...] = norms_ref[...] - jnp.sum(coeff_t * coeff_t, axis=1, keepdims=True)
    first = first_ref[0]
    count = projected_ref.shape[0]
    projected_ref[...] = projected_buf[pl.ds(first, count), :]
    picked = jnp.broadcast_to(residual_buf[pl.ds(first, count), :], (count, count))
    diagonal = lax.broadcasted_iota(jnp.int32, (count, count), 0) == lax.broadcasted_iota(jnp.int32, (count, count), 1)
    residual_ref[...] = jnp.sum(jnp.where(diagonal, picked, 0.0), axis=0, keepdims=True)


def rayleigh_ritz(first_band, band_count, margin, subspace, image_norms):
    size = margin.shape[0]
    return pl.pallas_call(
        rayleigh_ritz_kernel,
        out_shape=(jax.ShapeDtypeStruct((band_count, size), jnp.float32),
                   jax.ShapeDtypeStruct((1, band_count), jnp.float32)),
        in_specs=[pl.BlockSpec(memory_space=pltpu.SMEM)] + [pl.BlockSpec(memory_space=pltpu.VMEM)] * 3,
        out_specs=(pl.BlockSpec(memory_space=pltpu.VMEM), pl.BlockSpec(memory_space=pltpu.VMEM)),
        scratch_shapes=[pltpu.VMEM((size, size), jnp.float32), pltpu.VMEM((size, 1), jnp.float32)],
        cost_estimate=pl.CostEstimate(flops=6 * size**3, transcendentals=size, bytes_accessed=4 * 4 * size * size),
    )(first_band.reshape(1).astype(jnp.int32), margin, subspace, image_norms.reshape(size, 1))


def replica_pairs(direction):
    grid_count, band_count = lax.axis_size("grid"), lax.axis_size("band")
    pairs = []
    for target_grid in range(grid_count):
        source_grid = (target_grid - direction) % grid_count
        far = source_grid // 8 != target_grid // 8
        for target_band in range(band_count):
            source_band = target_band ^ 4 if far else target_band
            pairs.append((source_band * grid_count + source_grid, target_band * grid_count + target_grid))
    return pairs


def on_device(trial_bands, potential):
    band_count = trial_bands.shape[0]
    width = 2 * (filter_degree + 1)
    count = lax.axis_size("grid")
    below = lax.ppermute(trial_bands[:, trial_bands.shape[1] - width :], "grid", [(i, (i + 1) % count) for i in range(count)])
    above = lax.ppermute(trial_bands[:, :width], "grid", [((i + 1) % count, i) for i in range(count)])
    below_pot = lax.ppermute(potential[potential.shape[0] - width :], ("band", "grid"), replica_pairs(1))
    above_pot = lax.ppermute(potential[:width], ("band", "grid"), replica_pairs(-1))
    stacked = filter_and_image(below, trial_bands, above, below_pot, potential, above_pot)
    current = stacked[0]
    band_devices = lax.axis_size("band")
    total_bands = band_count * band_devices
    cell_count = current.shape[1] * current.shape[2] * current.shape[3]
    cell_total = cell_count * lax.axis_size("grid")
    inverse_cells = 1.0 / cell_total
    first_band = lax.axis_index("band") * band_count
    both = stacked.reshape(2, band_count, band_devices, cell_count // band_devices)
    moved = lax.all_to_all(both, "band", 2, 1, tiled=True)
    bands_here = moved[0].reshape(total_bands, -1)
    image_here = moved[1].reshape(total_bands, -1)
    margin_part = jnp.dot(
        bands_here, bands_here.T, precision=lax.Precision.HIGHEST, preferred_element_type=jnp.float32
    )
    image_part = jnp.dot(
        image_here, bands_here.T, precision=lax.Precision.HIGHEST, preferred_element_type=jnp.float32
    )
    norm_part = jnp.sum(image_here * image_here, axis=1)
    packed = jnp.concatenate([margin_part.reshape(-1), image_part.reshape(-1), norm_part])
    packed = butterfly_sum(packed, "band", [flip(1), flip(2), flip(4), flip(8), ring_of_four(0, 8)])
    packed = butterfly_sum(packed, "grid", [flip(1), flip(2), ring_of_four(0, 2), flip(8)])
    packed = packed * inverse_cells
    square = total_bands * total_bands
    margin = packed[:square].reshape(total_bands, total_bands)
    subspace = packed[square : 2 * square].reshape(total_bands, total_bands)
    image_norms = packed[2 * square :]
    margin = (margin + margin.T) / 2
    projected_rows, residual_rows = rayleigh_ritz(first_band, band_count, margin, subspace, image_norms)
    residual_rows = residual_rows.reshape(-1)
    return (current, projected_rows, residual_rows)


def solution(mesh):
    in_specs = (P("band", "grid", None, None), P("grid", None, None))
    out_specs = (P("band", "grid", None, None), P("band", None), P("band"))
    return jax.shard_map(
        on_device, mesh=mesh, in_specs=in_specs, out_specs=out_specs, check_vma=False
    )
```

```python
import functools

import jax
import jax.numpy as jnp
from jax import lax
from jax.experimental import pallas as pl
from jax.experimental.pallas import tpu as pltpu
from jax.sharding import PartitionSpec as P

CENTER = 4.25
HALF_WIDTH = 3.75
LOWEST = -2.0
SIGMA_ONE = HALF_WIDTH / (LOWEST - CENTER)
FOUR_THIRDS = 4.0 / 3.0
TWELFTH = 1.0 / 12.0
filter_degree = 4


def butterfly_sum(values, axis, partner_rounds):
    count = lax.axis_size(axis)
    for partner in partner_rounds:
        pairs = [(i, partner(i)) for i in range(count)]
        values = values + lax.ppermute(values, axis, pairs)
    return values


def flip(bit):
    return lambda i: i ^ bit


def ring_of_four(low, stride):
    def partner(i):
        place = (i // stride) % 4
        return i + (3 - 2 * place) * stride

    return partner


def filter_kernel(below_ref, own_ref, above_ref, below_pot, own_pot, above_pot, both_ref,
                  first_buf, second_buf, third_buf, wide_pot):
    band_count, own_planes = both_ref.shape[1], both_ref.shape[2]
    width = below_ref.shape[1]
    for at, source, pot in ((0, below_ref, below_pot), (width, own_ref, own_pot),
                            (width + own_planes, above_ref, above_pot)):
        first_buf[:, at : at + source.shape[1]] = source[...]
        wide_pot[at : at + source.shape[1]] = pot[...]
    rows, lanes = first_buf.shape[2], first_buf.shape[3]

    def apply(field, band, plane):
        centre = field[band, plane]
        near_sum = field[band, plane - 1] + field[band, plane + 1]
        near_sum = near_sum + pltpu.roll(centre, 1, 0) + pltpu.roll(centre, rows - 1, 0)
        near_sum = near_sum + pltpu.roll(centre, 1, 1) + pltpu.roll(centre, lanes - 1, 1)
        far_sum = field[band, plane - 2] + field[band, plane + 2]
        far_sum = far_sum + pltpu.roll(centre, 2, 0) + pltpu.roll(centre, rows - 2, 0)
        far_sum = far_sum + pltpu.roll(centre, 2, 1) + pltpu.roll(centre, lanes - 2, 1)
        kinetic = 0.5 * (7.5 * centre - FOUR_THIRDS * near_sum + TWELFTH * far_sum)
        return kinetic + wide_pot[plane] * centre, centre

    def sweep(field, older, out, lo, hi, scale, carry_scale):
        for plane in range(lo, hi):
            for band in range(band_count):
                applied, centre = apply(field, band, plane)
                value = (applied - CENTER * centre) * scale
                if older is not None:
                    value = value - carry_scale * older[band, plane]
                out[band, plane] = value

    total = first_buf.shape[1]
    sweep(first_buf, None, second_buf, 2, total - 2, SIGMA_ONE / HALF_WIDTH, 0.0)
    bufs = [first_buf, second_buf, third_buf]
    older, field, spare = 0, 1, 2
    sigma_now = SIGMA_ONE
    for repeat_index in range(filter_degree - 1):
        sigma_next = 1.0 / (2.0 / SIGMA_ONE - sigma_now)
        margin = 2 * (repeat_index + 2)
        sweep(bufs[field], bufs[older], bufs[spare], margin, total - margin,
              2.0 * sigma_next / HALF_WIDTH, sigma_now * sigma_next)
        older, field, spare = field, spare, older
        sigma_now = sigma_next
    final = bufs[field]
    both_ref[0] = final[:, width : width + own_planes]

    for plane in range(width, width + own_planes):
        for band in range(band_count):
            both_ref[1, band, plane - width], _ = apply(final, band, plane)


def filter_and_image(below, own, above, below_pot, own_pot, above_pot):
    band_count = own.shape[0]
    own_planes, rows, lanes = own.shape[1], own.shape[2], own.shape[3]
    total = below.shape[1] + own_planes + above.shape[1]
    shape = (band_count, own_planes, rows, lanes)
    cells = band_count * total * rows * lanes
    return pl.pallas_call(
        filter_kernel,
        out_shape=jax.ShapeDtypeStruct((2, *shape), jnp.float32),
        in_specs=[pl.BlockSpec(memory_space=pltpu.VMEM)] * 6,
        out_specs=pl.BlockSpec(memory_space=pltpu.VMEM),
        scratch_shapes=[pltpu.VMEM((band_count, total, rows, lanes), jnp.float32)] * 3
        + [pltpu.VMEM((total, rows, lanes), jnp.float32)],
        cost_estimate=pl.CostEstimate(flops=30 * cells * 4, transcendentals=0, bytes_accessed=4 * cells * 3),
    )(below, own, above, below_pot, own_pot, above_pot)


def rayleigh_ritz_kernel(scale, first_ref, packed_ref, projected_ref, residual_ref, projected_buf, residual_buf):
    size = packed_ref.shape[0]
    work = packed_ref[:, 0:size] * scale
    rest = packed_ref[:, 128 : 128 + size] * scale
    norms = packed_ref[:, 192:193] * scale
    rows = lax.broadcasted_iota(jnp.int32, (size, size), 0)
    cols = lax.broadcasted_iota(jnp.int32, (size, size), 1)
    row_index = rows[:, :1]
    col_index = cols[:1, :]
    coeff_t = jnp.zeros((size, size), jnp.float32)
    columns, inverses = [], []
    for k in range(size):
        inverse = 1.0 / jnp.sqrt(work[k : k + 1, k : k + 1])
        column = jnp.where(row_index >= k, work[:, k : k + 1] * inverse, 0.0)
        row = jnp.where(col_index >= k, work[k : k + 1, :] * inverse, 0.0)
        work = work - column * row
        solved = rest[:, k : k + 1] * inverse
        rest = rest - solved * jnp.where(col_index > k, row, 0.0)
        coeff_t = jnp.where(cols == k, solved, coeff_t)
        columns.append(jnp.where(row_index > k, column, 0.0))
        inverses.append(inverse)
    rest = coeff_t
    projected = jnp.zeros((size, size), jnp.float32)
    for i in range(size):
        row = rest[i : i + 1, :] * inverses[i]
        rest = rest - columns[i] * row
        projected = jnp.where(rows == i, row, projected)
    projected_buf[...] = projected
    residual_buf[...] = norms - jnp.sum(coeff_t * coeff_t, axis=1, keepdims=True)
    first = first_ref[0]
    count = projected_ref.shape[0]
    projected_ref[...] = projected_buf[pl.ds(first, count), :]
    picked = jnp.broadcast_to(residual_buf[pl.ds(first, count), :], (count, count))
    diagonal = lax.broadcasted_iota(jnp.int32, (count, count), 0) == lax.broadcasted_iota(jnp.int32, (count, count), 1)
    residual_ref[...] = jnp.sum(jnp.where(diagonal, picked, 0.0), axis=0, keepdims=True)


def rayleigh_ritz(first_band, band_count, packed, scale):
    size = packed.shape[0]
    return pl.pallas_call(
        functools.partial(rayleigh_ritz_kernel, scale),
        out_shape=(jax.ShapeDtypeStruct((band_count, size), jnp.float32),
                   jax.ShapeDtypeStruct((1, band_count), jnp.float32)),
        in_specs=[pl.BlockSpec(memory_space=pltpu.SMEM), pl.BlockSpec(memory_space=pltpu.VMEM)],
        out_specs=(pl.BlockSpec(memory_space=pltpu.VMEM), pl.BlockSpec(memory_space=pltpu.VMEM)),
        scratch_shapes=[pltpu.VMEM((size, size), jnp.float32), pltpu.VMEM((size, 1), jnp.float32)],
        cost_estimate=pl.CostEstimate(flops=6 * size**3, transcendentals=size, bytes_accessed=4 * 4 * size * size),
    )(first_band.reshape(1).astype(jnp.int32), packed)


def replica_pairs(direction):
    grid_count, band_count = lax.axis_size("grid"), lax.axis_size("band")
    pairs = []
    for target_grid in range(grid_count):
        source_grid = (target_grid - direction) % grid_count
        far = source_grid // 8 != target_grid // 8
        for target_band in range(band_count):
            source_band = target_band ^ 4 if far else target_band
            pairs.append((source_band * grid_count + source_grid, target_band * grid_count + target_grid))
    return pairs


def on_device(trial_bands, potential):
    band_count = trial_bands.shape[0]
    width = 2 * (filter_degree + 1)
    count = lax.axis_size("grid")
    below = lax.ppermute(trial_bands[:, trial_bands.shape[1] - width :], "grid", [(i, (i + 1) % count) for i in range(count)])
    above = lax.ppermute(trial_bands[:, :width], "grid", [((i + 1) % count, i) for i in range(count)])
    below_pot = lax.ppermute(potential[potential.shape[0] - width :], ("band", "grid"), replica_pairs(1))
    above_pot = lax.ppermute(potential[:width], ("band", "grid"), replica_pairs(-1))
    stacked = filter_and_image(below, trial_bands, above, below_pot, potential, above_pot)
    current = stacked[0]
    band_devices = lax.axis_size("band")
    total_bands = band_count * band_devices
    cell_count = current.shape[1] * current.shape[2] * current.shape[3]
    cell_total = cell_count * lax.axis_size("grid")
    inverse_cells = 1.0 / cell_total
    first_band = lax.axis_index("band") * band_count
    both = stacked.reshape(2, band_count, band_devices, cell_count // band_devices)
    moved = lax.all_to_all(both, "band", 2, 1, tiled=True)
    bands_here = moved[0].reshape(total_bands, -1)
    image_here = moved[1].reshape(total_bands, -1)
    margin_part = jnp.dot(
        bands_here, bands_here.T, precision=lax.Precision.HIGHEST, preferred_element_type=jnp.float32
    )
    image_part = jnp.dot(
        image_here, bands_here.T, precision=lax.Precision.HIGHEST, preferred_element_type=jnp.float32
    )
    norm_part = jnp.sum(image_here * image_here, axis=1)
    size = total_bands
    margin_part = (margin_part + margin_part.T) / 2
    packed = jnp.concatenate(
        [margin_part, jnp.zeros((size, 128 - size), jnp.float32), image_part, norm_part[:, None],
         jnp.zeros((size, 63), jnp.float32)],
        axis=1,
    )
    packed = butterfly_sum(packed, "band", [flip(1), flip(2), flip(4), flip(8), ring_of_four(0, 8)])
    packed = butterfly_sum(packed, "grid", [flip(1), flip(2), ring_of_four(0, 2), flip(8)])
    projected_rows, residual_rows = rayleigh_ritz(first_band, band_count, packed, inverse_cells)
    residual_rows = residual_rows.reshape(-1)
    return (current, projected_rows, residual_rows)


def solution(mesh):
    in_specs = (P("band", "grid", None, None), P("grid", None, None))
    out_specs = (P("band", "grid", None, None), P("band", None), P("band"))
    return jax.shard_map(
        on_device, mesh=mesh, in_specs=in_specs, out_specs=out_specs, check_vma=False
    )
```

```python
import jax
import jax.numpy as jnp
from jax import lax
from jax.experimental import pallas as pl
from jax.experimental.pallas import tpu as pltpu
from jax.sharding import PartitionSpec as P

CENTER = 4.25
HALF_WIDTH = 3.75
LOWEST = -2.0
SIGMA_ONE = HALF_WIDTH / (LOWEST - CENTER)
FOUR_THIRDS = 4.0 / 3.0
TWELFTH = 1.0 / 12.0
filter_degree = 4


def butterfly_sum(values, axis, partner_rounds):
    count = lax.axis_size(axis)
    for partner in partner_rounds:
        pairs = [(i, partner(i)) for i in range(count)]
        values = values + lax.ppermute(values, axis, pairs)
    return values


def flip(bit):
    return lambda i: i ^ bit


def ring_of_four(low, stride):
    def partner(i):
        place = (i // stride) % 4
        return i + (3 - 2 * place) * stride

    return partner


def filter_kernel(below_ref, own_ref, above_ref, below_pot, own_pot, above_pot, both_ref,
                  first_buf, second_buf, third_buf, wide_pot):
    band_count, own_planes = both_ref.shape[1], both_ref.shape[2]
    width = below_ref.shape[1]
    for at, source, pot in ((0, below_ref, below_pot), (width, own_ref, own_pot),
                            (width + own_planes, above_ref, above_pot)):
        first_buf[:, at : at + source.shape[1]] = source[...]
        wide_pot[at : at + source.shape[1]] = pot[...]
    rows, lanes = first_buf.shape[2], first_buf.shape[3]

    def apply(field, band, plane):
        centre = field[band, plane]
        near_sum = field[band, plane - 1] + field[band, plane + 1]
        near_sum = near_sum + pltpu.roll(centre, 1, 0) + pltpu.roll(centre, rows - 1, 0)
        near_sum = near_sum + pltpu.roll(centre, 1, 1) + pltpu.roll(centre, lanes - 1, 1)
        far_sum = field[band, plane - 2] + field[band, plane + 2]
        far_sum = far_sum + pltpu.roll(centre, 2, 0) + pltpu.roll(centre, rows - 2, 0)
        far_sum = far_sum + pltpu.roll(centre, 2, 1) + pltpu.roll(centre, lanes - 2, 1)
        kinetic = 0.5 * (7.5 * centre - FOUR_THIRDS * near_sum + TWELFTH * far_sum)
        return kinetic + wide_pot[plane] * centre, centre

    def sweep(field, older, out, lo, hi, scale, carry_scale):
        for plane in range(lo, hi):
            for band in range(band_count):
                applied, centre = apply(field, band, plane)
                value = (applied - CENTER * centre) * scale
                if older is not None:
                    value = value - carry_scale * older[band, plane]
                out[band, plane] = value

    total = first_buf.shape[1]
    sweep(first_buf, None, second_buf, 2, total - 2, SIGMA_ONE / HALF_WIDTH, 0.0)
    bufs = [first_buf, second_buf, third_buf]
    older, field, spare = 0, 1, 2
    sigma_now = SIGMA_ONE
    for repeat_index in range(filter_degree - 1):
        sigma_next = 1.0 / (2.0 / SIGMA_ONE - sigma_now)
        margin = 2 * (repeat_index + 2)
        sweep(bufs[field], bufs[older], bufs[spare], margin, total - margin,
              2.0 * sigma_next / HALF_WIDTH, sigma_now * sigma_next)
        older, field, spare = field, spare, older
        sigma_now = sigma_next
    final = bufs[field]
    both_ref[0] = final[:, width : width + own_planes]

    for plane in range(width, width + own_planes):
        for band in range(band_count):
            both_ref[1, band, plane - width], _ = apply(final, band, plane)


def filter_and_image(below, own, above, below_pot, own_pot, above_pot):
    band_count = own.shape[0]
    own_planes, rows, lanes = own.shape[1], own.shape[2], own.shape[3]
    total = below.shape[1] + own_planes + above.shape[1]
    shape = (band_count, own_planes, rows, lanes)
    cells = band_count * total * rows * lanes
    return pl.pallas_call(
        filter_kernel,
        out_shape=jax.ShapeDtypeStruct((2, *shape), jnp.float32),
        in_specs=[pl.BlockSpec(memory_space=pltpu.VMEM)] * 6,
        out_specs=pl.BlockSpec(memory_space=pltpu.VMEM),
        scratch_shapes=[pltpu.VMEM((band_count, total, rows, lanes), jnp.float32)] * 3
        + [pltpu.VMEM((total, rows, lanes), jnp.float32)],
        cost_estimate=pl.CostEstimate(flops=30 * cells * 4, transcendentals=0, bytes_accessed=4 * cells * 3),
    )(below, own, above, below_pot, own_pot, above_pot)


def rayleigh_ritz_kernel(first_ref, margin_ref, subspace_ref, norms_ref, projected_ref, residual_ref,
                         projected_buf, residual_buf):
    size = margin_ref.shape[0]
    work = margin_ref[...]
    rest = subspace_ref[...]
    rows = lax.broadcasted_iota(jnp.int32, (size, size), 0)
    cols = lax.broadcasted_iota(jnp.int32, (size, size), 1)
    row_index = rows[:, :1]
    col_index = cols[:1, :]
    coeff_t = jnp.zeros((size, size), jnp.float32)
    columns, inverses = [], []
    for k in range(size):
        inverse = 1.0 / jnp.sqrt(work[k : k + 1, k : k + 1])
        column = jnp.where(row_index >= k, work[:, k : k + 1] * inverse, 0.0)
        row = jnp.where(col_index >= k, work[k : k + 1, :] * inverse, 0.0)
        work = work - column * row
        solved = rest[:, k : k + 1] * inverse
        rest = rest - solved * jnp.where(col_index > k, row, 0.0)
        coeff_t = jnp.where(cols == k, solved, coeff_t)
        columns.append(jnp.where(row_index > k, column, 0.0))
        inverses.append(inverse)
    rest = coeff_t
    projected = jnp.zeros((size, size), jnp.float32)
    for i in range(size):
        row = rest[i : i + 1, :] * inverses[i]
        rest = rest - columns[i] * row
        projected = jnp.where(rows == i, row, projected)
    projected_buf[...] = projected
    residual_buf[...] = norms_ref[...] - jnp.sum(coeff_t * coeff_t, axis=1, keepdims=True)
    first = first_ref[0]
    count = projected_ref.shape[0]
    projected_ref[...] = projected_buf[pl.ds(first, count), :]
    picked = jnp.broadcast_to(residual_buf[pl.ds(first, count), :], (count, count))
    diagonal = lax.broadcasted_iota(jnp.int32, (count, count), 0) == lax.broadcasted_iota(jnp.int32, (count, count), 1)
    residual_ref[...] = jnp.sum(jnp.where(diagonal, picked, 0.0), axis=0, keepdims=True)


def rayleigh_ritz(first_band, band_count, margin, subspace, image_norms):
    size = margin.shape[0]
    return pl.pallas_call(
        rayleigh_ritz_kernel,
        out_shape=(jax.ShapeDtypeStruct((band_count, size), jnp.float32),
                   jax.ShapeDtypeStruct((1, band_count), jnp.float32)),
        in_specs=[pl.BlockSpec(memory_space=pltpu.SMEM)] + [pl.BlockSpec(memory_space=pltpu.VMEM)] * 3,
        out_specs=(pl.BlockSpec(memory_space=pltpu.VMEM), pl.BlockSpec(memory_space=pltpu.VMEM)),
        scratch_shapes=[pltpu.VMEM((size, size), jnp.float32), pltpu.VMEM((size, 1), jnp.float32)],
        cost_estimate=pl.CostEstimate(flops=6 * size**3, transcendentals=size, bytes_accessed=4 * 4 * size * size),
    )(first_band.reshape(1).astype(jnp.int32), margin, subspace, image_norms.reshape(size, 1))


def replica_pairs(direction):
    grid_count, band_count = lax.axis_size("grid"), lax.axis_size("band")
    pairs = []
    for target_grid in range(grid_count):
        source_grid = (target_grid - direction) % grid_count
        far = source_grid // 8 != target_grid // 8
        for target_band in range(band_count):
            source_band = target_band ^ 4 if far else target_band
            pairs.append((source_band * grid_count + source_grid, target_band * grid_count + target_grid))
    return pairs


def on_device(trial_bands, potential):
    band_count = trial_bands.shape[0]
    width = 2 * (filter_degree + 1)
    count = lax.axis_size("grid")
    below = lax.ppermute(trial_bands[:, trial_bands.shape[1] - width :], "grid", [(i, (i + 1) % count) for i in range(count)])
    above = lax.ppermute(trial_bands[:, :width], "grid", [((i + 1) % count, i) for i in range(count)])
    below_pot = lax.ppermute(potential[potential.shape[0] - width :], ("band", "grid"), replica_pairs(1))
    above_pot = lax.ppermute(potential[:width], ("band", "grid"), replica_pairs(-1))
    stacked = filter_and_image(below, trial_bands, above, below_pot, potential, above_pot)
    current = stacked[0]
    band_devices = lax.axis_size("band")
    total_bands = band_count * band_devices
    cell_count = current.shape[1] * current.shape[2] * current.shape[3]
    cell_total = cell_count * lax.axis_size("grid")
    inverse_cells = 1.0 / cell_total
    first_band = lax.axis_index("band") * band_count
    both = stacked.reshape(2, band_count, band_devices, cell_count // band_devices)
    moved = lax.all_to_all(both, "band", 2, 1, tiled=True)
    bands_here = moved[0].reshape(total_bands, -1)
    image_here = moved[1].reshape(total_bands, -1)
    margin_part = jnp.dot(
        bands_here, bands_here.T, precision=lax.Precision.HIGHEST, preferred_element_type=jnp.float32
    )
    image_part = jnp.dot(
        image_here, bands_here.T, precision=lax.Precision.HIGHEST, preferred_element_type=jnp.float32
    )
    norm_part = jnp.sum(image_here * image_here, axis=1)
    packed = jnp.concatenate([margin_part.reshape(-1), image_part.reshape(-1), norm_part])
    packed = butterfly_sum(packed, "band", [flip(1), flip(2), flip(4), flip(8), ring_of_four(0, 8)])
    packed = butterfly_sum(packed, "grid", [flip(2), ring_of_four(0, 2), flip(1), flip(8)])
    packed = packed * inverse_cells
    square = total_bands * total_bands
    margin = packed[:square].reshape(total_bands, total_bands)
    subspace = packed[square : 2 * square].reshape(total_bands, total_bands)
    image_norms = packed[2 * square :]
    margin = (margin + margin.T) / 2
    projected_rows, residual_rows = rayleigh_ritz(first_band, band_count, margin, subspace, image_norms)
    residual_rows = residual_rows.reshape(-1)
    return (current, projected_rows, residual_rows)


def solution(mesh):
    in_specs = (P("band", "grid", None, None), P("grid", None, None))
    out_specs = (P("band", "grid", None, None), P("band", None), P("band"))
    return jax.shard_map(
        on_device, mesh=mesh, in_specs=in_specs, out_specs=out_specs, check_vma=False
    )
```
